128 devices in a mesh: kv: 32 (over y, z, core), hd: 4 (over x).
Axes of the slice: x: 4, y: 4, z: 4, core: 2. Of those that a mesh axis runs over, the one named last changes fastest.
Arguments:
- kv_cache: bfloat16 [64, 16384, 256], P(None, 'kv'), may hold values from -6 to 6
- keep_lists: int32 [64, 16384], P(None, 'kv'), may hold values from 0 to 511, as said below
- kept_counts: int32 [64, 32], P(None, 'kv'), may hold values from 64 to 511
- drop_scores: float32 [64, 16384], P(None, 'kv'), may hold values from 0.01 to 10
- lengths: int32 [64], replicated, may hold values from 4096 to 16384, as said below
- offsets: int32 [64], replicated, may hold values from 0 to 31, as said below
- queries: bfloat16 [64, 2048], P(None, 'hd'), may hold values from -100 to 100
- out_weight: bfloat16 [2048, 2048], P('hd'), may hold values from -0.125 to 0.125
Outputs:
- projected: bfloat16 [64, 2048], P('kv', 'hd')
The draws below stay inside these ranges and needn't reach their ends.
Inputs may be any that keep to these rules, and one draw needn't show every extreme that they name: `keep_lists`: each aligned run of 512 entries is an ordering of 0 to 511. `lengths`: some request has length exactly 16384. `offsets`: exactly 32 requests have a nonzero offset; no nonzero value is taken by more than 2 requests, and one by exactly 2.
All inputs are finite; a program needn't handle non-finite values.
Results may differ from the reference program's by a relative error of at most 0.006.
Values may be sent and summed in bfloat16 or wider, within the bound.
No kernel may reach another device: no remote copies, remote signals or barrier semaphores. Data moves between devices by JAX's collectives and lax.ppermute only.
A program may use at most 128 MiB of HBM per device.

```python
import math
import jax
import jax.numpy as jnp
from jax import lax

D = 2048
HEADS = 16
HDIM = 128
BLK = 512
REQ = 64
CACHE = 16384
N_KV = 32


def draw_kv_cache(key, part):
    shape = (REQ, CACHE, 2 * HDIM)
    base = jnp.clip(jax.random.normal(jax.random.fold_in(key, 3), shape, jnp.float32), -6.0, 6.0)
    return base.astype(jnp.bfloat16)


def draw_queries(key, part):
    base = jnp.clip(jax.random.normal(jax.random.fold_in(key, 5), (REQ, D), jnp.float32), -6.0, 6.0)
    return base.astype(jnp.bfloat16)


def draw_keep_lists(key, part):
    subkeys = jax.random.split(jax.random.fold_in(key, 11), REQ * (CACHE // BLK))
    orders = jax.vmap(lambda single: jax.random.permutation(single, BLK))(subkeys)
    return orders.reshape(REQ, CACHE).astype(jnp.int32)


def draw_lengths(key, part):
    drawn = jax.random.randint(jax.random.fold_in(key, 13), (REQ,), CACHE // 4, CACHE + 1)
    chosen = jax.random.randint(jax.random.fold_in(key, 14), (), 0, REQ)
    return drawn.at[chosen].set(CACHE).astype(jnp.int32)


def draw_offsets(key, part):
    blocks = CACHE // BLK
    order = jax.random.permutation(jax.random.fold_in(key, 17), REQ)
    turn = jax.random.randint(jax.random.fold_in(key, 18), (), 0, blocks - 1)
    amounts = 1 + (jnp.arange(REQ // 2, dtype=jnp.int32) + turn) % (blocks - 1)
    return jnp.zeros((REQ,), jnp.int32).at[order[:REQ // 2]].set(amounts).astype(jnp.int32)


def place_ends(result, key, low, high):
    shape = result.shape
    place = [jax.random.randint(jax.random.fold_in(key, axis), (), 0, shape[axis]) for axis in range(len(shape))]
    result = result.at[tuple(place)].set(low)
    longest = shape.index(max(shape))
    place[longest] = (place[longest] + 1) % shape[longest]
    return result.at[tuple(place)].set(high)


def block_scale(stream_key, extent, shards, smallest, high):
    loudness = 1.0
    for axis_at, blocks in shards:
        heights = jax.random.uniform(jax.random.fold_in(jax.random.fold_in(stream_key, 6), axis_at), (blocks,), jnp.float32, smallest / len(shards), high / len(shards))
        loudness = loudness * jnp.repeat(jnp.exp(heights), extent[axis_at] // blocks).reshape((-1,) + (1,) * (len(extent) - 1 - axis_at))
    return loudness


def normal_values(key, extent, scale, bound, shards=(), kind=jnp.bfloat16):
    values = scale * jax.random.normal(key, extent, jnp.float32)
    if shards:
        values = values * block_scale(key, extent, shards, -0.22, 0.18)
    return jnp.clip(values, -bound, bound).astype(kind)


def setup_inputs(seed: int = 0) -> dict:
    key_list = jax.random.split(jax.random.key(seed), 9)
    kv_cache = draw_kv_cache(jax.random.fold_in(key_list[8], 71), 0)
    keep_lists = draw_keep_lists(jax.random.fold_in(key_list[8], 71), 0)
    kept_counts = place_ends(jax.random.randint(key_list[2], (REQ, N_KV), BLK // 8, BLK), jax.random.fold_in(key_list[2], 1), BLK // 8, BLK - 1).astype(jnp.int32)
    drop_scores = jnp.clip(jnp.exp(math.log(10.0) - 6.9077553 * jax.random.uniform(key_list[3], (REQ, CACHE), jnp.float32) ** block_scale(key_list[3], (REQ, CACHE), ((1, 32),), -0.2, 0.2)), 0.01, 10.0)
    lengths = draw_lengths(jax.random.fold_in(key_list[8], 71), 0)
    offsets = draw_offsets(jax.random.fold_in(key_list[8], 71), 0)
    queries = draw_queries(jax.random.fold_in(key_list[8], 71), 0)
    out_weight = normal_values(key_list[7], (D, D), D ** -0.5, 0.125, ((0, 4),))
    return dict(kv_cache=kv_cache, keep_lists=keep_lists, kept_counts=kept_counts, drop_scores=drop_scores, lengths=lengths, offsets=offsets, queries=queries, out_weight=out_weight)


def codes_for(keep_block, count_block, score_block, lengths, block_index):
    requests, block_rows = keep_block.shape
    row_index = jnp.arange(requests, dtype=jnp.int32)[:, None]
    places = jnp.broadcast_to(jnp.arange(block_rows, dtype=jnp.int32)[None, :], (requests, block_rows))
    rank_in_list = jnp.zeros((requests, block_rows), jnp.int32).at[row_index, keep_block].set(places)
    kept_rows = rank_in_list < count_block[:, None]
    position = block_index * block_rows + jnp.arange(block_rows, dtype=jnp.int32)
    valid_rows = position[None, :] < lengths[:, None]
    return jnp.where(valid_rows & kept_rows, -1.0, jnp.where(valid_rows, score_block, 0.0)).astype(jnp.float32)

def block_partial(block_data, codes, queries_h):
    head_dim = queries_h.shape[-1]
    factor = 1.0 / math.sqrt(head_dim)
    kept_rows = codes < 0.0
    weight = jnp.maximum(codes, 0.0)
    totals = lax.optimization_barrier(jnp.sum(weight, axis=1))
    has_merged = totals > 0.0
    floored = jnp.maximum(totals, 1.0)
    shares = (weight / floored[:, None]).astype(jnp.bfloat16)
    block_wide = block_data.astype(jnp.float32)
    merged = jnp.einsum('rb,rbc->rc', shares.astype(jnp.float32), block_wide).astype(jnp.bfloat16)
    merged_wide = merged.astype(jnp.float32)
    query_wide = queries_h.astype(jnp.float32)
    scores_qk = jnp.einsum('rhc,rbc->rhb', query_wide, block_wide[..., :head_dim]) * factor
    merged_score = jnp.einsum('rhc,rc->rh', query_wide, merged_wide[:, :head_dim]) * factor + jnp.log(floored)[:, None]
    scores_qk = jnp.where(kept_rows[:, None, :], scores_qk, -1e+30)
    merged_score = jnp.where(has_merged[:, None], merged_score, -1e+30)
    peaks = jnp.maximum(lax.optimization_barrier(jnp.max(scores_qk, axis=-1)), merged_score)
    probs = jnp.where(kept_rows[:, None, :], jnp.exp(scores_qk - peaks[..., None]), 0.0)
    merged_prob = jnp.where(has_merged[:, None], jnp.exp(merged_score - peaks), 0.0)
    mass = lax.optimization_barrier(jnp.sum(probs, axis=-1)) + merged_prob
    probs_low = lax.optimization_barrier(probs.astype(jnp.bfloat16))
    merged_low = lax.optimization_barrier(merged_prob.astype(jnp.bfloat16))
    weighted = jnp.einsum('rhb,rbc->rhc', probs_low.astype(jnp.float32), block_wide[..., head_dim:])
    weighted = weighted + merged_low.astype(jnp.float32)[..., None] * merged_wide[:, None, head_dim:]
    return (peaks, mass, weighted)

def reference(kv_cache, keep_lists, kept_counts, drop_scores, lengths, offsets, queries, out_weight):
    requests = kv_cache.shape[0]
    cube = kv_cache.reshape(requests, N_KV, BLK, 2 * HDIM)
    keep_cube = keep_lists.reshape(requests, N_KV, BLK)
    score_cube = drop_scores.reshape(requests, N_KV, BLK)
    queries_h = queries.reshape(requests, HEADS, HDIM)
    request_index = jnp.arange(requests, dtype=jnp.int32)

    def per_block(block_index):
        holder = ((block_index + offsets) % N_KV).astype(jnp.int32)
        block_data = cube[request_index, holder]
        keep_block = lax.dynamic_index_in_dim(keep_cube, block_index, 1, keepdims=False)
        count_block = lax.dynamic_index_in_dim(kept_counts, block_index, 1, keepdims=False)
        score_block = lax.dynamic_index_in_dim(score_cube, block_index, 1, keepdims=False)
        codes = codes_for(keep_block, count_block, score_block, lengths, block_index)
        return block_partial(block_data, codes, queries_h)
    peaks, mass, weighted = lax.map(per_block, jnp.arange(N_KV, dtype=jnp.int32))
    largest = lax.optimization_barrier(jnp.max(peaks, axis=0))
    factors = jnp.exp(peaks - largest[None])
    upper = lax.optimization_barrier(jnp.sum(factors[..., None] * weighted, axis=0))
    lower = lax.optimization_barrier(jnp.sum(factors * mass, axis=0))
    attended = (upper / lower[..., None]).astype(jnp.bfloat16).reshape(requests, HEADS * HDIM)
    return jnp.dot(attended, out_weight, preferred_element_type=jnp.float32).astype(jnp.bfloat16)
```

```python
import math

import jax
import jax.numpy as jnp
from jax import lax
from jax.sharding import PartitionSpec as P


def combined_all(value, axis, join):
    pieces = jax.tree.map(lambda part: lax.all_gather(part, axis), value)
    head = jax.tree.map(lambda part: part[0], pieces)
    tail = jax.tree.map(lambda part: part[1:], pieces)
    total, _ = lax.scan(lambda total, piece: (join(total, piece), None), head, tail)
    return total


def codes_for(keep_block, count_block, score_block, lengths, block_index):
    requests, block_rows = keep_block.shape
    row_index = jnp.arange(requests, dtype=jnp.int32)[:, None]
    places = jnp.broadcast_to(
        jnp.arange(block_rows, dtype=jnp.int32)[None, :], (requests, block_rows)
    )
    rank_in_list = (
        jnp.zeros((requests, block_rows), jnp.int32).at[row_index, keep_block].set(places)
    )
    kept_rows = rank_in_list < count_block[:, None]
    position = block_index * block_rows + jnp.arange(block_rows, dtype=jnp.int32)
    valid_rows = position[None, :] < lengths[:, None]
    return jnp.where(valid_rows & kept_rows, -1.0, jnp.where(valid_rows, score_block, 0.0))


def block_partial(block_data, codes, queries_h):
    head_dim = queries_h.shape[-1]
    factor = 1.0 / math.sqrt(head_dim)
    kept_rows = codes < 0.0
    weight = jnp.maximum(codes, 0.0)
    totals = jnp.sum(weight, axis=1)
    has_merged = totals > 0.0
    floored = jnp.maximum(totals, 1.0)
    shares = (weight / floored[:, None]).astype(jnp.bfloat16)
    merged = jnp.einsum(
        "rb,rbc->rc", shares, block_data, preferred_element_type=jnp.float32
    ).astype(jnp.bfloat16)
    scores_qk = (
        jnp.einsum(
            "rhc,rbc->rhb",
            queries_h,
            block_data[..., :head_dim],
            preferred_element_type=jnp.float32,
        )
        * factor
    )
    merged_score = (
        jnp.einsum(
            "rhc,rc->rh", queries_h, merged[:, :head_dim], preferred_element_type=jnp.float32
        )
        * factor
    )
    merged_score = merged_score + jnp.log(floored)[:, None]
    scores_qk = jnp.where(kept_rows[:, None, :], scores_qk, -1e30)
    merged_score = jnp.where(has_merged[:, None], merged_score, -1e30)
    peaks = jnp.maximum(jnp.max(scores_qk, axis=-1), merged_score)
    probs = jnp.where(kept_rows[:, None, :], jnp.exp(scores_qk - peaks[..., None]), 0.0)
    merged_prob = jnp.where(has_merged[:, None], jnp.exp(merged_score - peaks), 0.0)
    mass = jnp.sum(probs, axis=-1) + merged_prob
    weighted = jnp.einsum(
        "rhb,rbc->rhc",
        probs.astype(jnp.bfloat16),
        block_data[..., head_dim:],
        preferred_element_type=jnp.float32,
    )
    merged_value = merged[:, head_dim:].astype(jnp.float32)
    weighted = (
        weighted
        + merged_prob.astype(jnp.bfloat16).astype(jnp.float32)[..., None] * merged_value[:, None, :]
    )
    return (peaks, mass, weighted)


def route_tables(offsets, devices, capacity):
    requests = offsets.shape[0]
    one_hot = (offsets[:, None] == jnp.arange(devices, dtype=jnp.int32)[None, :]).astype(jnp.int32)
    position = jnp.sum(jnp.cumsum(one_hot, axis=0) * one_hot, axis=1) - 1
    table = (
        jnp.zeros((devices, capacity), jnp.int32)
        .at[offsets, position]
        .set(jnp.arange(requests, dtype=jnp.int32), mode="drop")
    )
    filled = jnp.zeros((devices, capacity), jnp.bool_).at[offsets, position].set(True, mode="drop")
    return (table, filled, position)


def pack_slots(values, table, filled, device, devices, direction):
    targets = jnp.arange(devices, dtype=jnp.int32)
    amount = direction * (device - targets) % devices
    chosen = table[amount]
    live_slots = filled[amount] & (amount != 0)[:, None]
    gathered = values[chosen]
    live_slots = live_slots.reshape(live_slots.shape + (1,) * (values.ndim - 1))
    return jnp.where(live_slots, gathered, jnp.zeros((), values.dtype))


def unpack_slots(received, values, offsets, position, device, devices, capacity, direction):
    source = (device + direction * offsets) % devices
    slots = source * capacity + jnp.minimum(position, capacity - 1)
    stacked = received.reshape((devices * capacity,) + received.shape[2:])
    taken = stacked[slots]
    moving = (offsets != 0).reshape((-1,) + (1,) * (values.ndim - 1))
    return jnp.where(moving, taken, values)


def join_partials(first, second):
    peak_one, mass_one, sum_one = first
    peak_two, mass_two, sum_two = second
    largest = jnp.maximum(peak_one, peak_two)
    scale_one = jnp.exp(peak_one - largest)
    scale_two = jnp.exp(peak_two - largest)
    return (
        largest,
        mass_one * scale_one + mass_two * scale_two,
        sum_one * scale_one[..., None] + sum_two * scale_two[..., None],
    )


def body(kv_cache, keep_lists, kept_counts, drop_scores, lengths, offsets, queries, out_weight):
    devices = lax.axis_size("kv")
    device = lax.axis_index("kv")
    requests, block_rows, width = kv_cache.shape
    head_dim = width // 2
    capacity = (requests // 2 + devices - 2) // (devices - 1)
    per_device = requests // devices
    codes = codes_for(keep_lists, kept_counts[:, 0], drop_scores, lengths, device)
    table, filled, position = route_tables(offsets, devices, capacity)
    outgoing = pack_slots(codes, table, filled, device, devices, -1)
    received = lax.all_to_all(outgoing, "kv", split_axis=0, concat_axis=0, tiled=True)
    held_codes = unpack_slots(received, codes, offsets, position, device, devices, capacity, -1)
    queries_h = queries.reshape(requests, -1, head_dim)
    peaks, mass, weighted = block_partial(kv_cache, held_codes, queries_h)
    largest = lax.pmax(peaks, "kv")
    scale = jnp.exp(peaks - largest)
    mass = mass * scale
    weighted = weighted * scale[..., None]
    mass_own = lax.psum_scatter(mass, "kv", scatter_dimension=0, tiled=True)
    weighted_own = lax.psum_scatter(weighted, "kv", scatter_dimension=0, tiled=True)
    attended = weighted_own / mass_own[..., None]
    attended = attended.astype(jnp.bfloat16).reshape(per_device, -1)
    partial_out = jnp.dot(attended, out_weight, preferred_element_type=jnp.float32)
    return lax.psum_scatter(partial_out, "hd", scatter_dimension=1, tiled=True).astype(jnp.bfloat16)


def solution(mesh):
    in_specs = (
        P(None, "kv", None),
        P(None, "kv"),
        P(None, "kv"),
        P(None, "kv"),
        P(),
        P(),
        P(None, "hd"),
        P("hd", None),
    )
    out_specs = P("kv", "hd")
    return jax.shard_map(body, mesh=mesh, in_specs=in_specs, out_specs=out_specs, check_vma=False)
```

```python
import math

import jax
import jax.numpy as jnp
from jax import lax
from jax.sharding import PartitionSpec as P


def combined_all(value, axis, join):
    pieces = jax.tree.map(lambda part: lax.all_gather(part, axis), value)
    head = jax.tree.map(lambda part: part[0], pieces)
    tail = jax.tree.map(lambda part: part[1:], pieces)
    total, _ = lax.scan(lambda total, piece: (join(total, piece), None), head, tail)
    return total


def codes_for(keep_block, count_block, score_block, lengths, block_index):
    requests, block_rows = keep_block.shape
    low = 32
    high = block_rows // low
    places = jnp.arange(block_rows, dtype=jnp.int32)[None, :]
    counted = (places < count_block[:, None]).astype(jnp.bfloat16)
    upper = (keep_block // low)[..., None] == jnp.arange(high, dtype=jnp.int32)
    lower = (keep_block % low)[..., None] == jnp.arange(low, dtype=jnp.int32)
    upper = upper.astype(jnp.bfloat16) * counted[..., None]
    lower = lower.astype(jnp.bfloat16)
    kept = jnp.einsum("rpa,rpb->rab", upper, lower, preferred_element_type=jnp.float32)
    kept_rows = kept.reshape(requests, block_rows) > 0.5
    position = block_index * block_rows + jnp.arange(block_rows, dtype=jnp.int32)
    valid_rows = position[None, :] < lengths[:, None]
    return jnp.where(valid_rows & kept_rows, -1.0, jnp.where(valid_rows, score_block, 0.0))


def block_partial(block_data, codes, queries_h):
    head_dim = queries_h.shape[-1]
    factor = 1.0 / math.sqrt(head_dim)
    kept_rows = codes < 0.0
    weight = jnp.maximum(codes, 0.0)
    totals = jnp.sum(weight, axis=1)
    has_merged = totals > 0.0
    floored = jnp.maximum(totals, 1.0)
    shares = (weight / floored[:, None]).astype(jnp.bfloat16)
    merged = jnp.einsum(
        "rb,rbc->rc", shares, block_data, preferred_element_type=jnp.float32
    ).astype(jnp.bfloat16)
    scores_qk = (
        jnp.einsum(
            "rhc,rbc->rhb",
            queries_h,
            block_data[..., :head_dim],
            preferred_element_type=jnp.float32,
        )
        * factor
    )
    merged_score = (
        jnp.einsum(
            "rhc,rc->rh", queries_h, merged[:, :head_dim], preferred_element_type=jnp.float32
        )
        * factor
    )
    merged_score = merged_score + jnp.log(floored)[:, None]
    scores_qk = jnp.where(kept_rows[:, None, :], scores_qk, -1e30)
    merged_score = jnp.where(has_merged[:, None], merged_score, -1e30)
    peaks = jnp.maximum(jnp.max(scores_qk, axis=-1), merged_score)
    probs = jnp.where(kept_rows[:, None, :], jnp.exp(scores_qk - peaks[..., None]), 0.0)
    merged_prob = jnp.where(has_merged[:, None], jnp.exp(merged_score - peaks), 0.0)
    mass = jnp.sum(probs, axis=-1) + merged_prob
    weighted = jnp.einsum(
        "rhb,rbc->rhc",
        probs.astype(jnp.bfloat16),
        block_data[..., head_dim:],
        preferred_element_type=jnp.float32,
    )
    merged_value = merged[:, head_dim:].astype(jnp.float32)
    weighted = (
        weighted
        + merged_prob.astype(jnp.bfloat16).astype(jnp.float32)[..., None] * merged_value[:, None, :]
    )
    return (peaks, mass, weighted)


def route_tables(offsets, devices, capacity):
    requests = offsets.shape[0]
    one_hot = (offsets[:, None] == jnp.arange(devices, dtype=jnp.int32)[None, :]).astype(jnp.int32)
    position = jnp.sum(jnp.cumsum(one_hot, axis=0) * one_hot, axis=1) - 1
    match = (offsets[:, None, None] == jnp.arange(devices, dtype=jnp.int32)[None, :, None]) & (
        position[:, None, None] == jnp.arange(capacity, dtype=jnp.int32)[None, None, :]
    )
    index = jnp.arange(requests, dtype=jnp.int32)[:, None, None]
    table = jnp.sum(jnp.where(match, index, 0), axis=0)
    filled = jnp.any(match, axis=0)
    return (table, filled, position)


def pack_slots(values, table, filled, device, devices, direction):
    targets = jnp.arange(devices, dtype=jnp.int32)
    amount = direction * (device - targets) % devices
    chosen = table[amount]
    live_slots = filled[amount] & (amount != 0)[:, None]
    gathered = values[chosen]
    live_slots = live_slots.reshape(live_slots.shape + (1,) * (values.ndim - 1))
    return jnp.where(live_slots, gathered, jnp.zeros((), values.dtype))


def unpack_slots(received, values, offsets, position, device, devices, capacity, direction):
    source = (device + direction * offsets) % devices
    slots = source * capacity + jnp.minimum(position, capacity - 1)
    stacked = received.reshape((devices * capacity,) + received.shape[2:])
    taken = stacked[slots]
    moving = (offsets != 0).reshape((-1,) + (1,) * (values.ndim - 1))
    return jnp.where(moving, taken, values)


def join_partials(first, second):
    peak_one, mass_one, sum_one = first
    peak_two, mass_two, sum_two = second
    largest = jnp.maximum(peak_one, peak_two)
    scale_one = jnp.exp(peak_one - largest)
    scale_two = jnp.exp(peak_two - largest)
    return (
        largest,
        mass_one * scale_one + mass_two * scale_two,
        sum_one * scale_one[..., None] + sum_two * scale_two[..., None],
    )


def body(kv_cache, keep_lists, kept_counts, drop_scores, lengths, offsets, queries, out_weight):
    devices = lax.axis_size("kv")
    device = lax.axis_index("kv")
    requests, block_rows, width = kv_cache.shape
    head_dim = width // 2
    capacity = (requests // 2 + devices - 2) // (devices - 1)
    per_device = requests // devices
    codes = codes_for(keep_lists, kept_counts[:, 0], drop_scores, lengths, device)
    table, filled, position = route_tables(offsets, devices, capacity)
    outgoing = pack_slots(codes, table, filled, device, devices, -1)
    received = lax.all_to_all(outgoing, "kv", split_axis=0, concat_axis=0, tiled=True)
    held_codes = unpack_slots(received, codes, offsets, position, device, devices, capacity, -1)
    queries_h = queries.reshape(requests, -1, head_dim)
    heads = queries_h.shape[1]
    peaks, mass, weighted = block_partial(kv_cache, held_codes, queries_h)
    stats = jnp.concatenate([peaks, mass], axis=1)
    stats = jnp.pad(stats, ((0, 0), (0, head_dim - 2 * heads)))
    payload = jnp.concatenate([weighted, stats[:, None, :]], axis=1)
    gathered = lax.all_to_all(payload, "kv", split_axis=0, concat_axis=0, tiled=True)
    gathered = gathered.reshape(devices, per_device, heads + 1, head_dim)
    sums = gathered[:, :, :heads, :]
    peaks_all = gathered[:, :, heads, :heads]
    mass_all = gathered[:, :, heads, heads : 2 * heads]
    largest = jnp.max(peaks_all, axis=0)
    factors = jnp.exp(peaks_all - largest[None])
    upper = jnp.sum(factors[..., None] * sums, axis=0)
    lower = jnp.sum(factors * mass_all, axis=0)
    attended = (upper / lower[..., None]).astype(jnp.bfloat16).reshape(per_device, -1)
    partial_out = jnp.dot(attended, out_weight, preferred_element_type=jnp.float32)
    groups = lax.axis_size("hd")
    pieces = partial_out.reshape(per_device, groups, -1).transpose(1, 0, 2)
    pieces = lax.all_to_all(pieces, "hd", split_axis=0, concat_axis=0, tiled=True)
    return jnp.sum(pieces, axis=0).astype(jnp.bfloat16)


def solution(mesh):
    in_specs = (
        P(None, "kv", None),
        P(None, "kv"),
        P(None, "kv"),
        P(None, "kv"),
        P(),
        P(),
        P(None, "hd"),
        P("hd", None),
    )
    out_specs = P("kv", "hd")
    return jax.shard_map(body, mesh=mesh, in_specs=in_specs, out_specs=out_specs, check_vma=False)
```

```python
import math

import jax
import jax.numpy as jnp
from jax import lax
from jax.sharding import PartitionSpec as P


def combined_all(value, axis, join):
    pieces = jax.tree.map(lambda part: lax.all_gather(part, axis), value)
    head = jax.tree.map(lambda part: part[0], pieces)
    tail = jax.tree.map(lambda part: part[1:], pieces)
    total, _ = lax.scan(lambda total, piece: (join(total, piece), None), head, tail)
    return total


def codes_for(keep_block, count_block, score_block, lengths, block_index):
    requests, block_rows = keep_block.shape
    low = 32
    high = block_rows // low
    places = jnp.arange(block_rows, dtype=jnp.int32)[None, :]
    counted = places < count_block[:, None]
    upper = (keep_block >> 5)[..., None] == jnp.arange(high, dtype=jnp.int32)
    lower = (keep_block & (low - 1))[..., None] == jnp.arange(low, dtype=jnp.int32)
    upper = (upper & counted[..., None]).astype(jnp.bfloat16)
    lower = lower.astype(jnp.bfloat16)
    kept = jnp.einsum("rpa,rpb->rab", upper, lower, preferred_element_type=jnp.float32)
    kept_rows = kept.reshape(requests, block_rows) > 0.5
    position = block_index * block_rows + jnp.arange(block_rows, dtype=jnp.int32)
    valid_rows = position[None, :] < lengths[:, None]
    return jnp.where(valid_rows & kept_rows, -1.0, jnp.where(valid_rows, score_block, 0.0))


def raw_scores(block_data, queries_h):
    head_dim = queries_h.shape[-1]
    factor = 1.0 / math.sqrt(head_dim)
    scores_qk = jnp.einsum(
        "rhc,rbc->rhb",
        queries_h,
        block_data[..., :head_dim],
        preferred_element_type=jnp.float32,
    )
    return lax.optimization_barrier(scores_qk * factor)


def block_partial(block_data, codes, queries_h, scores_qk):
    head_dim = queries_h.shape[-1]
    factor = 1.0 / math.sqrt(head_dim)
    kept_rows = codes < 0.0
    weight = jnp.maximum(codes, 0.0)
    totals = jnp.sum(weight, axis=1)
    has_merged = totals > 0.0
    floored = jnp.maximum(totals, 1.0)
    shares = (weight / floored[:, None]).astype(jnp.bfloat16)
    merged = jnp.einsum(
        "rb,rbc->rc", shares, block_data, preferred_element_type=jnp.float32
    ).astype(jnp.bfloat16)
    merged_score = (
        jnp.einsum(
            "rhc,rc->rh", queries_h, merged[:, :head_dim], preferred_element_type=jnp.float32
        )
        * factor
    )
    merged_score = merged_score + jnp.log(floored)[:, None]
    scores_qk = jnp.where(kept_rows[:, None, :], scores_qk, -1e30)
    merged_score = jnp.where(has_merged[:, None], merged_score, -1e30)
    peaks = jnp.maximum(jnp.max(scores_qk, axis=-1), merged_score)
    probs = jnp.where(kept_rows[:, None, :], jnp.exp(scores_qk - peaks[..., None]), 0.0)
    merged_prob = jnp.where(has_merged[:, None], jnp.exp(merged_score - peaks), 0.0)
    mass = jnp.sum(probs, axis=-1) + merged_prob
    weighted = jnp.einsum(
        "rhb,rbc->rhc",
        probs.astype(jnp.bfloat16),
        block_data[..., head_dim:],
        preferred_element_type=jnp.float32,
    )
    merged_value = merged[:, head_dim:].astype(jnp.float32)
    weighted = (
        weighted
        + merged_prob.astype(jnp.bfloat16).astype(jnp.float32)[..., None] * merged_value[:, None, :]
    )
    return (peaks, mass, weighted)


def route_tables(offsets, devices, capacity):
    requests = offsets.shape[0]
    index = jnp.arange(requests, dtype=jnp.int32)
    same = offsets[:, None] == offsets[None, :]
    position = jnp.sum((same & (index[None, :] < index[:, None])).astype(jnp.int32), axis=1)
    return position


def pack_slots(values, offsets, position, device, devices, capacity):
    requests = offsets.shape[0]
    index = jnp.arange(requests, dtype=jnp.int32)
    amount = (jnp.arange(devices, dtype=jnp.int32) - device) % devices
    match = (
        (offsets[None, None, :] == amount[:, None, None])
        & (position[None, None, :] == jnp.arange(capacity, dtype=jnp.int32)[None, :, None])
        & (amount != 0)[:, None, None]
    )
    chosen = jnp.sum(jnp.where(match, index, 0), axis=2)
    live = jnp.any(match, axis=2)
    gathered = values[chosen]
    return jnp.where(live[..., None], gathered, jnp.zeros((), values.dtype))


def unpack_slots(received, values, offsets, position, device, devices, capacity):
    source = (device - offsets) % devices
    slots = source * capacity + jnp.minimum(position, capacity - 1)
    stacked = received.reshape((devices * capacity,) + received.shape[2:])
    taken = stacked[slots]
    moving = (offsets != 0)[:, None]
    return jnp.where(moving, taken, values)


def join_partials(first, second):
    peak_one, mass_one, sum_one = first
    peak_two, mass_two, sum_two = second
    largest = jnp.maximum(peak_one, peak_two)
    scale_one = jnp.exp(peak_one - largest)
    scale_two = jnp.exp(peak_two - largest)
    return (
        largest,
        mass_one * scale_one + mass_two * scale_two,
        sum_one * scale_one[..., None] + sum_two * scale_two[..., None],
    )


def body(kv_cache, keep_lists, kept_counts, drop_scores, lengths, offsets, queries, out_weight):
    devices = lax.axis_size("kv")
    device = lax.axis_index("kv")
    requests, block_rows, width = kv_cache.shape
    head_dim = width // 2
    capacity = (requests // 2 + devices - 2) // (devices - 1)
    per_device = requests // devices
    codes = codes_for(keep_lists, kept_counts[:, 0], drop_scores, lengths, device)
    position = route_tables(offsets, devices, capacity)
    outgoing = pack_slots(codes, offsets, position, device, devices, capacity)
    received = lax.all_to_all(outgoing, "kv", split_axis=0, concat_axis=0, tiled=True)
    held_codes = unpack_slots(received, codes, offsets, position, device, devices, capacity)
    queries_h = queries.reshape(requests, -1, head_dim)
    heads = queries_h.shape[1]
    scores_qk = raw_scores(kv_cache, queries_h)
    peaks, mass, weighted = block_partial(kv_cache, held_codes, queries_h, scores_qk)
    stats = jnp.concatenate([peaks, mass], axis=1)
    stats = jnp.pad(stats, ((0, 0), (0, head_dim - 2 * heads)))
    payload = jnp.concatenate([weighted, stats[:, None, :]], axis=1)
    gathered = lax.all_to_all(payload, "kv", split_axis=0, concat_axis=0, tiled=True)
    gathered = gathered.reshape(devices, per_device, heads + 1, head_dim)
    sums = gathered[:, :, :heads, :]
    peaks_all = gathered[:, :, heads, :heads]
    mass_all = gathered[:, :, heads, heads : 2 * heads]
    largest = jnp.max(peaks_all, axis=0)
    factors = jnp.exp(peaks_all - largest[None])
    upper = jnp.sum(factors[..., None] * sums, axis=0)
    lower = jnp.sum(factors * mass_all, axis=0)
    attended = (upper / lower[..., None]).astype(jnp.bfloat16).reshape(per_device, -1)
    partial_out = jnp.dot(attended, out_weight, preferred_element_type=jnp.float32)
    groups = lax.axis_size("hd")
    pieces = partial_out.reshape(per_device, groups, -1).transpose(1, 0, 2)
    pieces = lax.all_to_all(pieces, "hd", split_axis=0, concat_axis=0, tiled=True)
    return jnp.sum(pieces, axis=0).astype(jnp.bfloat16)


def solution(mesh):
    in_specs = (
        P(None, "kv", None),
        P(None, "kv"),
        P(None, "kv"),
        P(None, "kv"),
        P(),
        P(),
        P(None, "hd"),
        P("hd", None),
    )
    out_specs = P("kv", "hd")
    return jax.shard_map(body, mesh=mesh, in_specs=in_specs, out_specs=out_specs, check_vma=False)
```

```python
import math

import jax
import jax.numpy as jnp
from jax import lax
from jax.sharding import PartitionSpec as P


def combined_all(value, axis, join):
    pieces = jax.tree.map(lambda part: lax.all_gather(part, axis), value)
    head = jax.tree.map(lambda part: part[0], pieces)
    tail = jax.tree.map(lambda part: part[1:], pieces)
    total, _ = lax.scan(lambda total, piece: (join(total, piece), None), head, tail)
    return total


def codes_for(keep_block, count_block, score_block, lengths, block_index):
    requests, block_rows = keep_block.shape
    low = 32
    high = block_rows // low
    places = jnp.arange(block_rows, dtype=jnp.int32)[None, :]
    counted = places < count_block[:, None]
    upper = (keep_block >> 5)[..., None] == jnp.arange(high, dtype=jnp.int32)
    lower = (keep_block & (low - 1))[..., None] == jnp.arange(low, dtype=jnp.int32)
    upper = (upper & counted[..., None]).astype(jnp.bfloat16)
    lower = lower.astype(jnp.bfloat16)
    kept = jnp.einsum("rpa,rpb->rab", upper, lower, preferred_element_type=jnp.float32)
    kept_rows = kept.reshape(requests, block_rows) > 0.5
    position = block_index * block_rows + jnp.arange(block_rows, dtype=jnp.int32)
    valid_rows = position[None, :] < lengths[:, None]
    return jnp.where(valid_rows & kept_rows, -1.0, jnp.where(valid_rows, score_block, 0.0))


def raw_scores(block_data, queries_h):
    head_dim = queries_h.shape[-1]
    factor = 1.0 / math.sqrt(head_dim)
    scores_qk = jnp.einsum(
        "rhc,rbc->rhb",
        queries_h,
        block_data[..., :head_dim],
        preferred_element_type=jnp.float32,
    )
    return lax.optimization_barrier(scores_qk * factor)


def block_partial(block_data, codes, queries_h, scores_qk):
    head_dim = queries_h.shape[-1]
    factor = 1.0 / math.sqrt(head_dim)
    kept_rows = codes < 0.0
    weight = jnp.maximum(codes, 0.0)
    totals = jnp.sum(weight, axis=1)
    has_merged = totals > 0.0
    floored = jnp.maximum(totals, 1.0)
    shares = (weight / floored[:, None]).astype(jnp.bfloat16)
    scores_qk = jnp.where(kept_rows[:, None, :], scores_qk, -1e30)
    kept_peaks = jnp.max(scores_qk, axis=-1)
    kept_probs = jnp.where(
        kept_rows[:, None, :], jnp.exp(scores_qk - kept_peaks[..., None]), 0.0
    )
    kept_mass = jnp.sum(kept_probs, axis=-1)
    rows = jnp.concatenate([shares[:, None, :], kept_probs.astype(jnp.bfloat16)], axis=1)
    products = jnp.einsum("rkb,rbc->rkc", rows, block_data, preferred_element_type=jnp.float32)
    merged = products[:, 0, :].astype(jnp.bfloat16)
    kept_weighted = products[:, 1:, head_dim:]
    merged_score = (
        jnp.einsum(
            "rhc,rc->rh", queries_h, merged[:, :head_dim], preferred_element_type=jnp.float32
        )
        * factor
    )
    merged_score = merged_score + jnp.log(floored)[:, None]
    merged_score = jnp.where(has_merged[:, None], merged_score, -1e30)
    peaks = jnp.maximum(kept_peaks, merged_score)
    rescale = jnp.exp(kept_peaks - peaks)
    merged_prob = jnp.where(has_merged[:, None], jnp.exp(merged_score - peaks), 0.0)
    mass = kept_mass * rescale + merged_prob
    merged_value = merged[:, head_dim:].astype(jnp.float32)
    weighted = (
        kept_weighted * rescale[..., None]
        + merged_prob.astype(jnp.bfloat16).astype(jnp.float32)[..., None] * merged_value[:, None, :]
    )
    return (peaks, mass, weighted)


def route_tables(offsets, devices, capacity):
    requests = offsets.shape[0]
    index = jnp.arange(requests, dtype=jnp.int32)
    same = offsets[:, None] == offsets[None, :]
    position = jnp.sum((same & (index[None, :] < index[:, None])).astype(jnp.int32), axis=1)
    return position


def pack_slots(values, offsets, position, device, devices, capacity):
    requests = offsets.shape[0]
    index = jnp.arange(requests, dtype=jnp.int32)
    amount = (jnp.arange(devices, dtype=jnp.int32) - device) % devices
    match = (
        (offsets[None, None, :] == amount[:, None, None])
        & (position[None, None, :] == jnp.arange(capacity, dtype=jnp.int32)[None, :, None])
        & (amount != 0)[:, None, None]
    )
    chosen = jnp.sum(jnp.where(match, index, 0), axis=2)
    live = jnp.any(match, axis=2)
    gathered = values[chosen]
    return jnp.where(live[..., None], gathered, jnp.zeros((), values.dtype))


def unpack_slots(received, values, offsets, position, device, devices, capacity):
    source = (device - offsets) % devices
    slots = source * capacity + jnp.minimum(position, capacity - 1)
    stacked = received.reshape((devices * capacity,) + received.shape[2:])
    taken = stacked[slots]
    moving = (offsets != 0)[:, None]
    return jnp.where(moving, taken, values)


def join_partials(first, second):
    peak_one, mass_one, sum_one = first
    peak_two, mass_two, sum_two = second
    largest = jnp.maximum(peak_one, peak_two)
    scale_one = jnp.exp(peak_one - largest)
    scale_two = jnp.exp(peak_two - largest)
    return (
        largest,
        mass_one * scale_one + mass_two * scale_two,
        sum_one * scale_one[..., None] + sum_two * scale_two[..., None],
    )


def body(kv_cache, keep_lists, kept_counts, drop_scores, lengths, offsets, queries, out_weight):
    devices = lax.axis_size("kv")
    device = lax.axis_index("kv")
    requests, block_rows, width = kv_cache.shape
    head_dim = width // 2
    capacity = (requests // 2 + devices - 2) // (devices - 1)
    per_device = requests // devices
    codes = codes_for(keep_lists, kept_counts[:, 0], drop_scores, lengths, device)
    position = route_tables(offsets, devices, capacity)
    outgoing = pack_slots(codes, offsets, position, device, devices, capacity)
    received = lax.all_to_all(outgoing, "kv", split_axis=0, concat_axis=0, tiled=True)
    held_codes = unpack_slots(received, codes, offsets, position, device, devices, capacity)
    queries_h = queries.reshape(requests, -1, head_dim)
    heads = queries_h.shape[1]
    scores_qk = raw_scores(kv_cache, queries_h)
    peaks, mass, weighted = block_partial(kv_cache, held_codes, queries_h, scores_qk)
    stats = jnp.concatenate([peaks, mass], axis=1)
    stats = jnp.pad(stats, ((0, 0), (0, head_dim - 2 * heads)))
    payload = jnp.concatenate([weighted, stats[:, None, :]], axis=1)
    gathered = lax.all_to_all(payload, "kv", split_axis=0, concat_axis=0, tiled=True)
    gathered = gathered.reshape(devices, per_device, heads + 1, head_dim)
    sums = gathered[:, :, :heads, :]
    peaks_all = gathered[:, :, heads, :heads]
    mass_all = gathered[:, :, heads, heads : 2 * heads]
    largest = jnp.max(peaks_all, axis=0)
    factors = jnp.exp(peaks_all - largest[None])
    upper = jnp.sum(factors[..., None] * sums, axis=0)
    lower = jnp.sum(factors * mass_all, axis=0)
    attended = (upper / lower[..., None]).astype(jnp.bfloat16).reshape(per_device, -1)
    partial_out = jnp.dot(attended, out_weight, preferred_element_type=jnp.float32)
    groups = lax.axis_size("hd")
    pieces = partial_out.reshape(per_device, groups, -1).transpose(1, 0, 2)
    pieces = lax.all_to_all(pieces, "hd", split_axis=0, concat_axis=0, tiled=True)
    return jnp.sum(pieces, axis=0).astype(jnp.bfloat16)


def solution(mesh):
    in_specs = (
        P(None, "kv", None),
        P(None, "kv"),
        P(None, "kv"),
        P(None, "kv"),
        P(),
        P(),
        P(None, "hd"),
        P("hd", None),
    )
    out_specs = P("kv", "hd")
    return jax.shard_map(body, mesh=mesh, in_specs=in_specs, out_specs=out_specs, check_vma=False)
```

```python
import math

import jax
import jax.numpy as jnp
from jax import lax
from jax.sharding import PartitionSpec as P


def combined_all(value, axis, join):
    pieces = jax.tree.map(lambda part: lax.all_gather(part, axis), value)
    head = jax.tree.map(lambda part: part[0], pieces)
    tail = jax.tree.map(lambda part: part[1:], pieces)
    total, _ = lax.scan(lambda total, piece: (join(total, piece), None), head, tail)
    return total


def codes_for(keep_block, count_block, score_block, lengths, block_index):
    requests, block_rows = keep_block.shape
    low = 32
    high = block_rows // low
    places = jnp.arange(block_rows, dtype=jnp.int32)[None, :]
    counted = places < count_block[:, None]
    upper = (keep_block >> 5)[..., None] == jnp.arange(high, dtype=jnp.int32)
    lower = (keep_block & (low - 1))[..., None] == jnp.arange(low, dtype=jnp.int32)
    upper = (upper & counted[..., None]).astype(jnp.bfloat16)
    lower = lower.astype(jnp.bfloat16)
    kept = jnp.einsum("rpa,rpb->rab", upper, lower, preferred_element_type=jnp.float32)
    kept_rows = kept.reshape(requests, block_rows) > 0.5
    position = block_index * block_rows + jnp.arange(block_rows, dtype=jnp.int32)
    valid_rows = position[None, :] < lengths[:, None]
    return jnp.where(valid_rows & kept_rows, -1.0, jnp.where(valid_rows, score_block, 0.0))


def raw_scores(block_data, queries_h):
    head_dim = queries_h.shape[-1]
    factor = 1.0 / math.sqrt(head_dim)
    scores_qk = jnp.einsum(
        "rhc,rbc->rhb",
        queries_h,
        block_data[..., :head_dim],
        preferred_element_type=jnp.float32,
    )
    return lax.optimization_barrier(scores_qk * factor)


def block_partial(block_data, codes, queries_h, scores_qk):
    head_dim = queries_h.shape[-1]
    factor = 1.0 / math.sqrt(head_dim)
    kept_rows = codes < 0.0
    weight = jnp.maximum(codes, 0.0)
    totals = jnp.sum(weight, axis=1)
    has_merged = totals > 0.0
    floored = jnp.maximum(totals, 1.0)
    shares = (weight / floored[:, None]).astype(jnp.bfloat16)
    scores_qk = jnp.where(kept_rows[:, None, :], scores_qk, -1e30)
    kept_peaks = jnp.max(scores_qk, axis=-1)
    kept_probs = jnp.where(
        kept_rows[:, None, :], jnp.exp(scores_qk - kept_peaks[..., None]), 0.0
    )
    kept_mass = jnp.sum(kept_probs, axis=-1)
    rows = jnp.concatenate([shares[:, None, :], kept_probs.astype(jnp.bfloat16)], axis=1)
    products = jnp.einsum("rkb,rbc->rkc", rows, block_data, preferred_element_type=jnp.float32)
    merged = products[:, 0, :].astype(jnp.bfloat16)
    kept_weighted = products[:, 1:, head_dim:]
    merged_score = (
        jnp.einsum(
            "rhc,rc->rh", queries_h, merged[:, :head_dim], preferred_element_type=jnp.float32
        )
        * factor
    )
    merged_score = merged_score + jnp.log(floored)[:, None]
    merged_score = jnp.where(has_merged[:, None], merged_score, -1e30)
    peaks = jnp.maximum(kept_peaks, merged_score)
    rescale = jnp.exp(kept_peaks - peaks)
    merged_prob = jnp.where(has_merged[:, None], jnp.exp(merged_score - peaks), 0.0)
    mass = kept_mass * rescale + merged_prob
    merged_value = merged[:, head_dim:].astype(jnp.float32)
    weighted = (
        kept_weighted * rescale[..., None]
        + merged_prob.astype(jnp.bfloat16).astype(jnp.float32)[..., None] * merged_value[:, None, :]
    )
    return (peaks, mass, weighted)


def route_tables(offsets, devices, capacity):
    requests = offsets.shape[0]
    index = jnp.arange(requests, dtype=jnp.int32)
    same = offsets[:, None] == offsets[None, :]
    position = jnp.sum((same & (index[None, :] < index[:, None])).astype(jnp.int32), axis=1)
    return position


def pack_slots(values, offsets, device, devices):
    requests = offsets.shape[0]
    index = jnp.arange(requests, dtype=jnp.int32)
    amount = (jnp.arange(devices, dtype=jnp.int32) - device) % devices
    match = (offsets[None, :] == amount[:, None]) & (amount != 0)[:, None]
    first = jnp.min(jnp.where(match, index, requests), axis=1)
    last = jnp.max(jnp.where(match, index, -1), axis=1)
    zero = jnp.zeros((), values.dtype)
    lower = jnp.where((first < requests)[:, None], values[jnp.minimum(first, requests - 1)], zero)
    upper = jnp.where((last > first)[:, None], values[jnp.maximum(last, 0)], zero)
    return jnp.stack([lower, upper], axis=1)


def unpack_slots(received, values, offsets, position, device, devices, capacity):
    source = (device - offsets) % devices
    slots = source * capacity + jnp.minimum(position, capacity - 1)
    stacked = received.reshape((devices * capacity,) + received.shape[2:])
    taken = stacked[slots]
    moving = (offsets != 0)[:, None]
    return jnp.where(moving, taken, values)


def join_partials(first, second):
    peak_one, mass_one, sum_one = first
    peak_two, mass_two, sum_two = second
    largest = jnp.maximum(peak_one, peak_two)
    scale_one = jnp.exp(peak_one - largest)
    scale_two = jnp.exp(peak_two - largest)
    return (
        largest,
        mass_one * scale_one + mass_two * scale_two,
        sum_one * scale_one[..., None] + sum_two * scale_two[..., None],
    )


def body(kv_cache, keep_lists, kept_counts, drop_scores, lengths, offsets, queries, out_weight):
    devices = lax.axis_size("kv")
    device = lax.axis_index("kv")
    requests, block_rows, width = kv_cache.shape
    head_dim = width // 2
    capacity = (requests // 2 + devices - 2) // (devices - 1)
    per_device = requests // devices
    codes = codes_for(keep_lists, kept_counts[:, 0], drop_scores, lengths, device)
    outgoing = pack_slots(codes, offsets, device, devices)
    received = lax.all_to_all(outgoing, "kv", split_axis=0, concat_axis=0, tiled=True)
    position = route_tables(offsets, devices, capacity)
    held_codes = unpack_slots(received, codes, offsets, position, device, devices, capacity)
    queries_h = queries.reshape(requests, -1, head_dim)
    heads = queries_h.shape[1]
    scores_qk = raw_scores(kv_cache, queries_h)
    peaks, mass, weighted = block_partial(kv_cache, held_codes, queries_h, scores_qk)
    stats = jnp.concatenate([peaks, mass], axis=1)
    stats = jnp.pad(stats, ((0, 0), (0, head_dim - 2 * heads)))
    payload = jnp.concatenate([weighted, stats[:, None, :]], axis=1)
    gathered = lax.all_to_all(payload, "kv", split_axis=0, concat_axis=0, tiled=True)
    gathered = gathered.reshape(devices, per_device, heads + 1, head_dim)
    sums = gathered[:, :, :heads, :]
    peaks_all = gathered[:, :, heads, :heads]
    mass_all = gathered[:, :, heads, heads : 2 * heads]
    largest = jnp.max(peaks_all, axis=0)
    factors = jnp.exp(peaks_all - largest[None])
    upper = jnp.sum(factors[..., None] * sums, axis=0)
    lower = jnp.sum(factors * mass_all, axis=0)
    attended = (upper / lower[..., None]).astype(jnp.bfloat16).reshape(per_device, -1)
    partial_out = jnp.dot(attended, out_weight, preferred_element_type=jnp.float32)
    groups = lax.axis_size("hd")
    pieces = partial_out.reshape(per_device, groups, -1).transpose(1, 0, 2)
    pieces = lax.all_to_all(pieces, "hd", split_axis=0, concat_axis=0, tiled=True)
    return jnp.sum(pieces, axis=0).astype(jnp.bfloat16)


def solution(mesh):
    in_specs = (
        P(None, "kv", None),
        P(None, "kv"),
        P(None, "kv"),
        P(None, "kv"),
        P(),
        P(),
        P(None, "hd"),
        P("hd", None),
    )
    out_specs = P("kv", "hd")
    return jax.shard_map(body, mesh=mesh, in_specs=in_specs, out_specs=out_specs, check_vma=False)
```

```python
import math

import jax
import jax.numpy as jnp
from jax import lax
from jax.sharding import PartitionSpec as P


def combined_all(value, axis, join):
    pieces = jax.tree.map(lambda part: lax.all_gather(part, axis), value)
    head = jax.tree.map(lambda part: part[0], pieces)
    tail = jax.tree.map(lambda part: part[1:], pieces)
    total, _ = lax.scan(lambda total, piece: (join(total, piece), None), head, tail)
    return total


def codes_for(keep_block, count_block, score_block, lengths, block_index):
    requests, block_rows = keep_block.shape
    low = 32
    high = block_rows // low
    places = jnp.arange(block_rows, dtype=jnp.int32)[None, :]
    counted = places < count_block[:, None]
    upper = (keep_block >> 5)[..., None] == jnp.arange(high, dtype=jnp.int32)
    lower = (keep_block & (low - 1))[..., None] == jnp.arange(low, dtype=jnp.int32)
    upper = (upper & counted[..., None]).astype(jnp.bfloat16)
    lower = lower.astype(jnp.bfloat16)
    kept = jnp.einsum("rpa,rpb->rab", upper, lower, preferred_element_type=jnp.float32)
    kept_rows = kept.reshape(requests, block_rows) > 0.5
    position = block_index * block_rows + jnp.arange(block_rows, dtype=jnp.int32)
    valid_rows = position[None, :] < lengths[:, None]
    return jnp.where(valid_rows & kept_rows, -1.0, jnp.where(valid_rows, score_block, 0.0))


def raw_scores(block_data, queries_h):
    head_dim = queries_h.shape[-1]
    factor = 1.0 / math.sqrt(head_dim)
    scores_qk = jnp.einsum(
        "rhc,rbc->rhb",
        queries_h,
        block_data[..., :head_dim],
        preferred_element_type=jnp.float32,
    )
    return lax.optimization_barrier(scores_qk * factor)


def block_partial(block_data, codes, queries_h, scores_qk):
    head_dim = queries_h.shape[-1]
    factor = 1.0 / math.sqrt(head_dim)
    kept_rows = codes < 0.0
    weight = jnp.maximum(codes, 0.0)
    totals = jnp.sum(weight, axis=1)
    has_merged = totals > 0.0
    floored = jnp.maximum(totals, 1.0)
    shares = (weight / floored[:, None]).astype(jnp.bfloat16)
    scores_qk = jnp.where(kept_rows[:, None, :], scores_qk, -1e30)
    kept_peaks = jnp.max(scores_qk, axis=-1)
    kept_probs = jnp.where(
        kept_rows[:, None, :], jnp.exp(scores_qk - kept_peaks[..., None]), 0.0
    )
    kept_mass = jnp.sum(kept_probs, axis=-1)
    rows = jnp.concatenate([shares[:, None, :], kept_probs.astype(jnp.bfloat16)], axis=1)
    products = jnp.einsum("rkb,rbc->rkc", rows, block_data, preferred_element_type=jnp.float32)
    merged = products[:, 0, :].astype(jnp.bfloat16)
    kept_weighted = products[:, 1:, head_dim:]
    merged_score = (
        jnp.einsum(
            "rhc,rc->rh", queries_h, merged[:, :head_dim], preferred_element_type=jnp.float32
        )
        * factor
    )
    merged_score = merged_score + jnp.log(floored)[:, None]
    merged_score = jnp.where(has_merged[:, None], merged_score, -1e30)
    peaks = jnp.maximum(kept_peaks, merged_score)
    rescale = jnp.exp(kept_peaks - peaks)
    merged_prob = jnp.where(has_merged[:, None], jnp.exp(merged_score - peaks), 0.0)
    mass = kept_mass * rescale + merged_prob
    merged_value = merged[:, head_dim:].astype(jnp.float32)
    weighted = (
        kept_weighted * rescale[..., None]
        + merged_prob.astype(jnp.bfloat16).astype(jnp.float32)[..., None] * merged_value[:, None, :]
    )
    return (peaks, mass, weighted)


def route_tables(offsets, devices, capacity):
    requests = offsets.shape[0]
    index = jnp.arange(requests, dtype=jnp.int32)
    same = offsets[:, None] == offsets[None, :]
    position = jnp.sum((same & (index[None, :] < index[:, None])).astype(jnp.int32), axis=1)
    return position


def pack_slots(values, offsets, device, devices, capacity):
    requests = offsets.shape[0]
    index = jnp.arange(requests, dtype=jnp.int32)
    slot_ids = jnp.arange(devices * capacity, dtype=jnp.int32)
    amount = (slot_ids // capacity - device) % devices
    second = (slot_ids % capacity) == 1
    match = (offsets[None, :] == amount[:, None]) & (amount != 0)[:, None]
    first = jnp.min(jnp.where(match, index, requests), axis=1)
    last = jnp.max(jnp.where(match, index, -1), axis=1)
    chosen = jnp.clip(jnp.where(second, last, first), 0, requests - 1)
    live = jnp.where(second, last > first, first < requests)
    return jnp.where(live[:, None], values[chosen], jnp.zeros((), values.dtype))


def unpack_slots(received, values, offsets, position, device, devices, capacity):
    source = (device - offsets) % devices
    slots = source * capacity + jnp.minimum(position, capacity - 1)
    taken = received[slots]
    moving = (offsets != 0)[:, None]
    return jnp.where(moving, taken, values)


def join_partials(first, second):
    peak_one, mass_one, sum_one = first
    peak_two, mass_two, sum_two = second
    largest = jnp.maximum(peak_one, peak_two)
    scale_one = jnp.exp(peak_one - largest)
    scale_two = jnp.exp(peak_two - largest)
    return (
        largest,
        mass_one * scale_one + mass_two * scale_two,
        sum_one * scale_one[..., None] + sum_two * scale_two[..., None],
    )


def body(kv_cache, keep_lists, kept_counts, drop_scores, lengths, offsets, queries, out_weight):
    devices = lax.axis_size("kv")
    device = lax.axis_index("kv")
    requests, block_rows, width = kv_cache.shape
    head_dim = width // 2
    capacity = (requests // 2 + devices - 2) // (devices - 1)
    per_device = requests // devices
    codes = codes_for(keep_lists, kept_counts[:, 0], drop_scores, lengths, device)
    outgoing = pack_slots(codes, offsets, device, devices, capacity)
    received = lax.all_to_all(outgoing, "kv", split_axis=0, concat_axis=0, tiled=True)
    position = route_tables(offsets, devices, capacity)
    held_codes = unpack_slots(received, codes, offsets, position, device, devices, capacity)
    queries_h = queries.reshape(requests, -1, head_dim)
    heads = queries_h.shape[1]
    scores_qk = raw_scores(kv_cache, queries_h)
    peaks, mass, weighted = block_partial(kv_cache, held_codes, queries_h, scores_qk)
    stats = jnp.concatenate([peaks, mass], axis=1)
    stats = jnp.pad(stats, ((0, 0), (0, head_dim - 2 * heads)))
    payload = jnp.concatenate([weighted, stats[:, None, :]], axis=1)
    gathered = lax.all_to_all(payload, "kv", split_axis=0, concat_axis=0, tiled=True)
    gathered = gathered.reshape(devices, per_device, heads + 1, head_dim)
    sums = gathered[:, :, :heads, :]
    peaks_all = gathered[:, :, heads, :heads]
    mass_all = gathered[:, :, heads, heads : 2 * heads]
    largest = jnp.max(peaks_all, axis=0)
    factors = jnp.exp(peaks_all - largest[None])
    upper = jnp.sum(factors[..., None] * sums, axis=0)
    lower = jnp.sum(factors * mass_all, axis=0)
    attended = (upper / lower[..., None]).astype(jnp.bfloat16).reshape(per_device, -1)
    partial_out = jnp.dot(attended, out_weight, preferred_element_type=jnp.float32)
    groups = lax.axis_size("hd")
    pieces = partial_out.reshape(per_device, groups, -1).transpose(1, 0, 2)
    pieces = lax.all_to_all(pieces, "hd", split_axis=0, concat_axis=0, tiled=True)
    return jnp.sum(pieces, axis=0).astype(jnp.bfloat16)


def solution(mesh):
    in_specs = (
        P(None, "kv", None),
        P(None, "kv"),
        P(None, "kv"),
        P(None, "kv"),
        P(),
        P(),
        P(None, "hd"),
        P("hd", None),
    )
    out_specs = P("kv", "hd")
    return jax.shard_map(body, mesh=mesh, in_specs=in_specs, out_specs=out_specs, check_vma=False)
```

```python
import math

import jax
import jax.numpy as jnp
from jax import lax
from jax.sharding import PartitionSpec as P


def combined_all(value, axis, join):
    pieces = jax.tree.map(lambda part: lax.all_gather(part, axis), value)
    head = jax.tree.map(lambda part: part[0], pieces)
    tail = jax.tree.map(lambda part: part[1:], pieces)
    total, _ = lax.scan(lambda total, piece: (join(total, piece), None), head, tail)
    return total


def codes_for(keep_block, count_block, score_block, lengths, block_index):
    requests, block_rows = keep_block.shape
    low = 32
    high = block_rows // low
    places = jnp.arange(block_rows, dtype=jnp.int32)[None, :]
    counted_hi = jnp.where(places < count_block[:, None], keep_block >> 5, -1)
    upper = (counted_hi[..., None] == jnp.arange(high, dtype=jnp.int32)).astype(jnp.bfloat16)
    lower = ((keep_block & (low - 1))[..., None] == jnp.arange(low, dtype=jnp.int32)).astype(
        jnp.bfloat16
    )
    kept = jnp.einsum("rpa,rpb->rab", upper, lower, preferred_element_type=jnp.float32)
    kept_rows = kept.reshape(requests, block_rows) > 0.5
    position = block_index * block_rows + jnp.arange(block_rows, dtype=jnp.int32)
    valid_rows = position[None, :] < lengths[:, None]
    return jnp.where(valid_rows & kept_rows, -1.0, jnp.where(valid_rows, score_block, 0.0))


def raw_scores(block_data, queries_h):
    head_dim = queries_h.shape[-1]
    factor = 1.0 / math.sqrt(head_dim)
    scores_qk = jnp.einsum(
        "rhc,rbc->rhb",
        queries_h,
        block_data[..., :head_dim],
        preferred_element_type=jnp.float32,
    )
    return lax.optimization_barrier(scores_qk * factor)


def block_partial(block_data, codes, queries_h, scores_qk):
    head_dim = queries_h.shape[-1]
    factor = 1.0 / math.sqrt(head_dim)
    kept_rows = codes < 0.0
    weight = jnp.maximum(codes, 0.0)
    totals = jnp.sum(weight, axis=1)
    has_merged = totals > 0.0
    floored = jnp.maximum(totals, 1.0)
    shares = (weight / floored[:, None]).astype(jnp.bfloat16)
    scores_qk = jnp.where(kept_rows[:, None, :], scores_qk, -1e30)
    kept_peaks = jnp.max(scores_qk, axis=-1)
    kept_probs = jnp.where(
        kept_rows[:, None, :], jnp.exp(scores_qk - kept_peaks[..., None]), 0.0
    )
    kept_mass = jnp.sum(kept_probs, axis=-1)
    rows = jnp.concatenate([shares[:, None, :], kept_probs.astype(jnp.bfloat16)], axis=1)
    products = jnp.einsum("rkb,rbc->rkc", rows, block_data, preferred_element_type=jnp.float32)
    merged = products[:, 0, :].astype(jnp.bfloat16)
    kept_weighted = products[:, 1:, head_dim:]
    merged_score = (
        jnp.einsum(
            "rhc,rc->rh", queries_h, merged[:, :head_dim], preferred_element_type=jnp.float32
        )
        * factor
    )
    merged_score = merged_score + jnp.log(floored)[:, None]
    merged_score = jnp.where(has_merged[:, None], merged_score, -1e30)
    peaks = jnp.maximum(kept_peaks, merged_score)
    rescale = jnp.exp(kept_peaks - peaks)
    merged_prob = jnp.where(has_merged[:, None], jnp.exp(merged_score - peaks), 0.0)
    mass = kept_mass * rescale + merged_prob
    merged_value = merged[:, head_dim:].astype(jnp.float32)
    weighted = (
        kept_weighted * rescale[..., None]
        + merged_prob.astype(jnp.bfloat16).astype(jnp.float32)[..., None] * merged_value[:, None, :]
    )
    return (peaks, mass, weighted)


def route_tables(offsets, devices, capacity):
    requests = offsets.shape[0]
    index = jnp.arange(requests, dtype=jnp.int32)
    same = offsets[:, None] == offsets[None, :]
    position = jnp.sum((same & (index[None, :] < index[:, None])).astype(jnp.int32), axis=1)
    return position


def pack_slots(values, offsets, device, devices, capacity):
    requests = offsets.shape[0]
    index = jnp.arange(requests, dtype=jnp.int32)
    slot_ids = jnp.arange(devices * capacity, dtype=jnp.int32)
    amount = (slot_ids // capacity - device) % devices
    second = (slot_ids % capacity) == 1
    match = (offsets[None, :] == amount[:, None]) & (amount != 0)[:, None]
    first = jnp.min(jnp.where(match, index, requests), axis=1)
    last = jnp.max(jnp.where(match, index, -1), axis=1)
    chosen = jnp.clip(jnp.where(second, last, first), 0, requests - 1)
    live = jnp.where(second, last > first, first < requests)
    return jnp.where(live[:, None], values[chosen], jnp.zeros((), values.dtype))


def unpack_slots(received, values, offsets, position, device, devices, capacity):
    source = (device - offsets) % devices
    slots = source * capacity + jnp.minimum(position, capacity - 1)
    taken = received[slots]
    moving = (offsets != 0)[:, None]
    return jnp.where(moving, taken, values)


def join_partials(first, second):
    peak_one, mass_one, sum_one = first
    peak_two, mass_two, sum_two = second
    largest = jnp.maximum(peak_one, peak_two)
    scale_one = jnp.exp(peak_one - largest)
    scale_two = jnp.exp(peak_two - largest)
    return (
        largest,
        mass_one * scale_one + mass_two * scale_two,
        sum_one * scale_one[..., None] + sum_two * scale_two[..., None],
    )


def body(kv_cache, keep_lists, kept_counts, drop_scores, lengths, offsets, queries, out_weight):
    devices = lax.axis_size("kv")
    device = lax.axis_index("kv")
    requests, block_rows, width = kv_cache.shape
    head_dim = width // 2
    capacity = (requests // 2 + devices - 2) // (devices - 1)
    per_device = requests // devices
    codes = codes_for(keep_lists, kept_counts[:, 0], drop_scores, lengths, device)
    outgoing = pack_slots(codes, offsets, device, devices, capacity)
    received = lax.all_to_all(outgoing, "kv", split_axis=0, concat_axis=0, tiled=True)
    position = route_tables(offsets, devices, capacity)
    held_codes = unpack_slots(received, codes, offsets, position, device, devices, capacity)
    queries_h = queries.reshape(requests, -1, head_dim)
    heads = queries_h.shape[1]
    scores_qk = raw_scores(kv_cache, queries_h)
    peaks, mass, weighted = block_partial(kv_cache, held_codes, queries_h, scores_qk)
    stats = jnp.concatenate([peaks, mass], axis=1)
    stats = jnp.pad(stats, ((0, 0), (0, head_dim - 2 * heads)))
    payload = jnp.concatenate([weighted, stats[:, None, :]], axis=1)
    gathered = lax.all_to_all(payload, "kv", split_axis=0, concat_axis=0, tiled=True)
    gathered = gathered.reshape(devices, per_device, heads + 1, head_dim)
    sums = gathered[:, :, :heads, :]
    peaks_all = gathered[:, :, heads, :heads]
    mass_all = gathered[:, :, heads, heads : 2 * heads]
    largest = jnp.max(peaks_all, axis=0)
    factors = jnp.exp(peaks_all - largest[None])
    upper = jnp.sum(factors[..., None] * sums, axis=0)
    lower = jnp.sum(factors * mass_all, axis=0)
    attended = (upper / lower[..., None]).astype(jnp.bfloat16).reshape(per_device, -1)
    partial_out = jnp.dot(attended, out_weight, preferred_element_type=jnp.float32)
    groups = lax.axis_size("hd")
    pieces = partial_out.reshape(per_device, groups, -1).transpose(1, 0, 2)
    pieces = lax.all_to_all(pieces, "hd", split_axis=0, concat_axis=0, tiled=True)
    return jnp.sum(pieces, axis=0).astype(jnp.bfloat16)


def solution(mesh):
    in_specs = (
        P(None, "kv", None),
        P(None, "kv"),
        P(None, "kv"),
        P(None, "kv"),
        P(),
        P(),
        P(None, "hd"),
        P("hd", None),
    )
    out_specs = P("kv", "hd")
    return jax.shard_map(body, mesh=mesh, in_specs=in_specs, out_specs=out_specs, check_vma=False)
```

```python
import math

import jax
import jax.numpy as jnp
from jax import lax
from jax.sharding import PartitionSpec as P


def combined_all(value, axis, join):
    pieces = jax.tree.map(lambda part: lax.all_gather(part, axis), value)
    head = jax.tree.map(lambda part: part[0], pieces)
    tail = jax.tree.map(lambda part: part[1:], pieces)
    total, _ = lax.scan(lambda total, piece: (join(total, piece), None), head, tail)
    return total


def codes_for(keep_block, count_block, score_block, lengths, block_index):
    requests, block_rows = keep_block.shape
    low = 32
    high = block_rows // low
    places = jnp.arange(block_rows, dtype=jnp.int32)[None, :]
    counted_hi = jnp.where(places < count_block[:, None], keep_block >> 5, -1)
    upper = (counted_hi[..., None] == jnp.arange(high, dtype=jnp.int32)).astype(jnp.bfloat16)
    lower = ((keep_block & (low - 1))[..., None] == jnp.arange(low, dtype=jnp.int32)).astype(
        jnp.bfloat16
    )
    kept = jnp.einsum("rpa,rpb->rab", upper, lower, preferred_element_type=jnp.float32)
    kept_rows = kept.reshape(requests, block_rows) > 0.5
    position = block_index * block_rows + jnp.arange(block_rows, dtype=jnp.int32)
    valid_rows = position[None, :] < lengths[:, None]
    return jnp.where(valid_rows & kept_rows, -1.0, jnp.where(valid_rows, score_block, 0.0))


def raw_scores(block_data, queries_h):
    head_dim = queries_h.shape[-1]
    factor = 1.0 / math.sqrt(head_dim)
    scores_qk = jnp.einsum(
        "rhc,rbc->rhb",
        queries_h,
        block_data[..., :head_dim],
        preferred_element_type=jnp.float32,
    )
    return lax.optimization_barrier(scores_qk * factor)


def block_partial(block_data, codes, queries_h, scores_qk):
    head_dim = queries_h.shape[-1]
    factor = 1.0 / math.sqrt(head_dim)
    kept_rows = codes < 0.0
    weight = jnp.maximum(codes, 0.0)
    totals = jnp.sum(weight, axis=1)
    has_merged = totals > 0.0
    floored = jnp.maximum(totals, 1.0)
    shares = (weight / floored[:, None]).astype(jnp.bfloat16)
    scores_qk = jnp.where(kept_rows[:, None, :], scores_qk, -1e30)
    kept_peaks = jnp.max(scores_qk, axis=-1)
    kept_probs = jnp.where(
        kept_rows[:, None, :], jnp.exp(scores_qk - kept_peaks[..., None]), 0.0
    )
    kept_mass = jnp.sum(kept_probs, axis=-1)
    rows = jnp.concatenate([shares[:, None, :], kept_probs.astype(jnp.bfloat16)], axis=1)
    products = jnp.einsum("rkb,rbc->rkc", rows, block_data, preferred_element_type=jnp.float32)
    merged = products[:, 0, :].astype(jnp.bfloat16)
    kept_weighted = products[:, 1:, head_dim:]
    merged_score = (
        jnp.einsum(
            "rhc,rc->rh", queries_h, merged[:, :head_dim], preferred_element_type=jnp.float32
        )
        * factor
    )
    merged_score = merged_score + jnp.log(floored)[:, None]
    merged_score = jnp.where(has_merged[:, None], merged_score, -1e30)
    peaks = jnp.maximum(kept_peaks, merged_score)
    rescale = jnp.exp(kept_peaks - peaks)
    merged_prob = jnp.where(has_merged[:, None], jnp.exp(merged_score - peaks), 0.0)
    mass = kept_mass * rescale + merged_prob
    merged_value = merged[:, head_dim:].astype(jnp.float32)
    weighted = (
        kept_weighted * rescale[..., None]
        + merged_prob.astype(jnp.bfloat16).astype(jnp.float32)[..., None] * merged_value[:, None, :]
    )
    return (peaks, mass, weighted)


def route_tables(offsets, devices, capacity):
    requests = offsets.shape[0]
    index = jnp.arange(requests, dtype=jnp.int32)
    same = offsets[:, None] == offsets[None, :]
    position = jnp.sum((same & (index[None, :] < index[:, None])).astype(jnp.int32), axis=1)
    return position


def pack_slots(values, offsets, device, devices, capacity):
    requests = offsets.shape[0]
    index = jnp.arange(requests, dtype=jnp.int32)
    slot_ids = jnp.arange(devices * capacity, dtype=jnp.int32)
    amount = (slot_ids // capacity - device) % devices
    second = (slot_ids % capacity) == 1
    same = offsets[:, None] == offsets[None, :]
    earlier = jnp.sum((same & (index[None, :] < index[:, None])).astype(jnp.int32), axis=1)
    match = (
        (offsets[None, :] == amount[:, None])
        & (amount != 0)[:, None]
        & ((earlier[None, :] == 1) == second[:, None])
    )
    return jnp.dot(match.astype(values.dtype), values, precision=lax.Precision.HIGHEST)


def unpack_slots(received, values, offsets, position, device, devices, capacity):
    source = (device - offsets) % devices
    slots = source * capacity + jnp.minimum(position, capacity - 1)
    taken = received[slots]
    moving = (offsets != 0)[:, None]
    return jnp.where(moving, taken, values)


def join_partials(first, second):
    peak_one, mass_one, sum_one = first
    peak_two, mass_two, sum_two = second
    largest = jnp.maximum(peak_one, peak_two)
    scale_one = jnp.exp(peak_one - largest)
    scale_two = jnp.exp(peak_two - largest)
    return (
        largest,
        mass_one * scale_one + mass_two * scale_two,
        sum_one * scale_one[..., None] + sum_two * scale_two[..., None],
    )


def body(kv_cache, keep_lists, kept_counts, drop_scores, lengths, offsets, queries, out_weight):
    devices = lax.axis_size("kv")
    device = lax.axis_index("kv")
    requests, block_rows, width = kv_cache.shape
    head_dim = width // 2
    capacity = (requests // 2 + devices - 2) // (devices - 1)
    per_device = requests // devices
    codes = codes_for(keep_lists, kept_counts[:, 0], drop_scores, lengths, device)
    outgoing = pack_slots(codes, offsets, device, devices, capacity)
    received = lax.all_to_all(outgoing, "kv", split_axis=0, concat_axis=0, tiled=True)
    position = route_tables(offsets, devices, capacity)
    held_codes = unpack_slots(received, codes, offsets, position, device, devices, capacity)
    queries_h = queries.reshape(requests, -1, head_dim)
    heads = queries_h.shape[1]
    scores_qk = raw_scores(kv_cache, queries_h)
    peaks, mass, weighted = block_partial(kv_cache, held_codes, queries_h, scores_qk)
    stats = jnp.concatenate([peaks, mass], axis=1)
    stats = jnp.pad(stats, ((0, 0), (0, head_dim - 2 * heads)))
    payload = jnp.concatenate([weighted, stats[:, None, :]], axis=1)
    gathered = lax.all_to_all(payload, "kv", split_axis=0, concat_axis=0, tiled=True)
    gathered = gathered.reshape(devices, per_device, heads + 1, head_dim)
    sums = gathered[:, :, :heads, :]
    peaks_all = gathered[:, :, heads, :heads]
    mass_all = gathered[:, :, heads, heads : 2 * heads]
    largest = jnp.max(peaks_all, axis=0)
    factors = jnp.exp(peaks_all - largest[None])
    upper = jnp.sum(factors[..., None] * sums, axis=0)
    lower = jnp.sum(factors * mass_all, axis=0)
    attended = (upper / lower[..., None]).astype(jnp.bfloat16).reshape(per_device, -1)
    partial_out = jnp.dot(attended, out_weight, preferred_element_type=jnp.float32)
    groups = lax.axis_size("hd")
    pieces = partial_out.reshape(per_device, groups, -1).transpose(1, 0, 2)
    pieces = lax.all_to_all(pieces, "hd", split_axis=0, concat_axis=0, tiled=True)
    return jnp.sum(pieces, axis=0).astype(jnp.bfloat16)


def solution(mesh):
    in_specs = (
        P(None, "kv", None),
        P(None, "kv"),
        P(None, "kv"),
        P(None, "kv"),
        P(),
        P(),
        P(None, "hd"),
        P("hd", None),
    )
    out_specs = P("kv", "hd")
    return jax.shard_map(body, mesh=mesh, in_specs=in_specs, out_specs=out_specs, check_vma=False)
```

```python
import math

import jax
import jax.numpy as jnp
from jax import lax
from jax.sharding import PartitionSpec as P


def combined_all(value, axis, join):
    pieces = jax.tree.map(lambda part: lax.all_gather(part, axis), value)
    head = jax.tree.map(lambda part: part[0], pieces)
    tail = jax.tree.map(lambda part: part[1:], pieces)
    total, _ = lax.scan(lambda total, piece: (join(total, piece), None), head, tail)
    return total


def codes_for(keep_block, count_block, score_block, lengths, block_index):
    requests, block_rows = keep_block.shape
    low = 32
    high = block_rows // low
    places = jnp.arange(block_rows, dtype=jnp.int32)[None, :]
    counted_hi = jnp.where(places < count_block[:, None], keep_block >> 5, -1)
    upper = (counted_hi[..., None] == jnp.arange(high, dtype=jnp.int32)).astype(jnp.bfloat16)
    lower = ((keep_block & (low - 1))[..., None] == jnp.arange(low, dtype=jnp.int32)).astype(
        jnp.bfloat16
    )
    kept = jnp.einsum("rpa,rpb->rab", upper, lower, preferred_element_type=jnp.float32)
    kept_rows = kept.reshape(requests, block_rows) > 0.5
    position = block_index * block_rows + jnp.arange(block_rows, dtype=jnp.int32)
    valid_rows = position[None, :] < lengths[:, None]
    return jnp.where(valid_rows & kept_rows, -1.0, jnp.where(valid_rows, score_block, 0.0))


def raw_scores(block_data, queries_h):
    head_dim = queries_h.shape[-1]
    factor = 1.0 / math.sqrt(head_dim)
    scores_qk = jnp.einsum(
        "rhc,rbc->rhb",
        queries_h,
        block_data[..., :head_dim],
        preferred_element_type=jnp.float32,
    )
    return lax.optimization_barrier(scores_qk * factor)


def block_partial(block_data, codes, queries_h, scores_qk):
    head_dim = queries_h.shape[-1]
    factor = 1.0 / math.sqrt(head_dim)
    kept_rows = codes < 0.0
    weight = jnp.maximum(codes, 0.0)
    totals = jnp.sum(weight, axis=1)
    has_merged = totals > 0.0
    floored = jnp.maximum(totals, 1.0)
    shares = (weight / floored[:, None]).astype(jnp.bfloat16)
    scores_qk = jnp.where(kept_rows[:, None, :], scores_qk, -1e30)
    kept_peaks = jnp.max(scores_qk, axis=-1)
    kept_probs = jnp.where(
        kept_rows[:, None, :], jnp.exp(scores_qk - kept_peaks[..., None]), 0.0
    )
    kept_mass = jnp.sum(kept_probs, axis=-1)
    rows = jnp.concatenate([shares[:, None, :], kept_probs.astype(jnp.bfloat16)], axis=1)
    products = jnp.einsum("rkb,rbc->rkc", rows, block_data, preferred_element_type=jnp.float32)
    merged = products[:, 0, :].astype(jnp.bfloat16)
    kept_weighted = products[:, 1:, head_dim:]
    merged_score = (
        jnp.einsum(
            "rhc,rc->rh", queries_h, merged[:, :head_dim], preferred_element_type=jnp.float32
        )
        * factor
    )
    merged_score = merged_score + jnp.log(floored)[:, None]
    merged_score = jnp.where(has_merged[:, None], merged_score, -1e30)
    peaks = jnp.maximum(kept_peaks, merged_score)
    rescale = jnp.exp(kept_peaks - peaks)
    merged_prob = jnp.where(has_merged[:, None], jnp.exp(merged_score - peaks), 0.0)
    mass = kept_mass * rescale + merged_prob
    merged_value = merged[:, head_dim:].astype(jnp.float32)
    weighted = (
        kept_weighted * rescale[..., None]
        + merged_prob.astype(jnp.bfloat16).astype(jnp.float32)[..., None] * merged_value[:, None, :]
    )
    return (peaks, mass, weighted)


def route_tables(offsets, devices, capacity):
    requests = offsets.shape[0]
    index = jnp.arange(requests, dtype=jnp.int32)
    same = offsets[:, None] == offsets[None, :]
    position = jnp.sum((same & (index[None, :] < index[:, None])).astype(jnp.int32), axis=1)
    return position


def pack_slots(values, offsets, device, devices, capacity):
    requests = offsets.shape[0]
    index = jnp.arange(requests, dtype=jnp.int32)
    slot_ids = jnp.arange(devices * capacity, dtype=jnp.int32)
    amount = (slot_ids // capacity - device) % devices
    second = (slot_ids % capacity) == 1
    same = offsets[:, None] == offsets[None, :]
    earlier = jnp.sum((same & (index[None, :] < index[:, None])).astype(jnp.int32), axis=1)
    match = (
        (offsets[None, :] == amount[:, None])
        & (amount != 0)[:, None]
        & ((earlier[None, :] == 1) == second[:, None])
    )
    return jnp.dot(match.astype(values.dtype), values, precision=lax.Precision.HIGHEST)


def unpack_slots(received, values, offsets, position, device, devices, capacity):
    source = (device - offsets) % devices
    slots = source * capacity + jnp.minimum(position, capacity - 1)
    moving = offsets != 0
    flat = received.reshape(devices * capacity, -1)
    picks = (slots[:, None] == jnp.arange(devices * capacity, dtype=jnp.int32)[None, :]) & moving[:, None]
    taken = jnp.dot(picks.astype(values.dtype), flat, precision=lax.Precision.HIGHEST)
    return taken + jnp.where(moving[:, None], jnp.zeros((), values.dtype), values)


def join_partials(first, second):
    peak_one, mass_one, sum_one = first
    peak_two, mass_two, sum_two = second
    largest = jnp.maximum(peak_one, peak_two)
    scale_one = jnp.exp(peak_one - largest)
    scale_two = jnp.exp(peak_two - largest)
    return (
        largest,
        mass_one * scale_one + mass_two * scale_two,
        sum_one * scale_one[..., None] + sum_two * scale_two[..., None],
    )


def body(kv_cache, keep_lists, kept_counts, drop_scores, lengths, offsets, queries, out_weight):
    devices = lax.axis_size("kv")
    device = lax.axis_index("kv")
    requests, block_rows, width = kv_cache.shape
    head_dim = width // 2
    capacity = (requests // 2 + devices - 2) // (devices - 1)
    per_device = requests // devices
    codes = codes_for(keep_lists, kept_counts[:, 0], drop_scores, lengths, device)
    outgoing = pack_slots(codes, offsets, device, devices, capacity)
    received = lax.all_to_all(outgoing, "kv", split_axis=0, concat_axis=0, tiled=True)
    position = route_tables(offsets, devices, capacity)
    held_codes = unpack_slots(received, codes, offsets, position, device, devices, capacity)
    queries_h = queries.reshape(requests, -1, head_dim)
    heads = queries_h.shape[1]
    scores_qk = raw_scores(kv_cache, queries_h)
    peaks, mass, weighted = block_partial(kv_cache, held_codes, queries_h, scores_qk)
    stats = jnp.concatenate([peaks, mass], axis=1)
    stats = jnp.pad(stats, ((0, 0), (0, head_dim - 2 * heads)))
    payload = jnp.concatenate([weighted, stats[:, None, :]], axis=1)
    gathered = lax.all_to_all(payload, "kv", split_axis=0, concat_axis=0, tiled=True)
    gathered = gathered.reshape(devices, per_device, heads + 1, head_dim)
    sums = gathered[:, :, :heads, :]
    peaks_all = gathered[:, :, heads, :heads]
    mass_all = gathered[:, :, heads, heads : 2 * heads]
    largest = jnp.max(peaks_all, axis=0)
    factors = jnp.exp(peaks_all - largest[None])
    upper = jnp.sum(factors[..., None] * sums, axis=0)
    lower = jnp.sum(factors * mass_all, axis=0)
    attended = (upper / lower[..., None]).astype(jnp.bfloat16).reshape(per_device, -1)
    partial_out = jnp.dot(attended, out_weight, preferred_element_type=jnp.float32)
    groups = lax.axis_size("hd")
    pieces = partial_out.reshape(per_device, groups, -1).transpose(1, 0, 2)
    pieces = lax.all_to_all(pieces, "hd", split_axis=0, concat_axis=0, tiled=True)
    return jnp.sum(pieces, axis=0).astype(jnp.bfloat16)


def solution(mesh):
    in_specs = (
        P(None, "kv", None),
        P(None, "kv"),
        P(None, "kv"),
        P(None, "kv"),
        P(),
        P(),
        P(None, "hd"),
        P("hd", None),
    )
    out_specs = P("kv", "hd")
    return jax.shard_map(body, mesh=mesh, in_specs=in_specs, out_specs=out_specs, check_vma=False)
```

```python
import math

import jax
import jax.numpy as jnp
from jax import lax
from jax.sharding import PartitionSpec as P


def combined_all(value, axis, join):
    pieces = jax.tree.map(lambda part: lax.all_gather(part, axis), value)
    head = jax.tree.map(lambda part: part[0], pieces)
    tail = jax.tree.map(lambda part: part[1:], pieces)
    total, _ = lax.scan(lambda total, piece: (join(total, piece), None), head, tail)
    return total


def codes_for(keep_block, count_block, score_block, lengths, block_index):
    requests, block_rows = keep_block.shape
    low = 32
    high = block_rows // low
    places = jnp.arange(block_rows, dtype=jnp.int32)[None, :]
    counted_hi = jnp.where(places < count_block[:, None], keep_block >> 5, -1)
    upper = (counted_hi[..., None] == jnp.arange(high, dtype=jnp.int32)).astype(jnp.bfloat16)
    lower = ((keep_block & (low - 1))[..., None] == jnp.arange(low, dtype=jnp.int32)).astype(
        jnp.bfloat16
    )
    kept = jnp.einsum("rpa,rpb->rab", upper, lower, preferred_element_type=jnp.float32)
    kept_rows = kept.reshape(requests, block_rows) > 0.5
    position = block_index * block_rows + jnp.arange(block_rows, dtype=jnp.int32)
    valid_rows = position[None, :] < lengths[:, None]
    return jnp.where(valid_rows & kept_rows, -1.0, jnp.where(valid_rows, score_block, 0.0))


def raw_scores(block_data, queries_h):
    head_dim = queries_h.shape[-1]
    factor = 1.0 / math.sqrt(head_dim)
    scores_qk = jnp.einsum(
        "rhc,rbc->rhb",
        queries_h,
        block_data[..., :head_dim],
        preferred_element_type=jnp.float32,
    )
    return lax.optimization_barrier(scores_qk * factor)


def block_partial(block_data, codes, queries_h, scores_qk):
    head_dim = queries_h.shape[-1]
    factor = 1.0 / math.sqrt(head_dim)
    kept_rows = codes < 0.0
    weight = jnp.maximum(codes, 0.0)
    totals = jnp.sum(weight, axis=1)
    has_merged = totals > 0.0
    floored = jnp.maximum(totals, 1.0)
    shares = (weight / floored[:, None]).astype(jnp.bfloat16)
    raw_qk = scores_qk
    scores_qk = jnp.where(kept_rows[:, None, :], scores_qk, -1e30)
    kept_peaks = jnp.max(scores_qk, axis=-1)
    kept_probs = jnp.where(
        kept_rows[:, None, :], jnp.exp(scores_qk - kept_peaks[..., None]), 0.0
    )
    kept_mass = jnp.sum(kept_probs, axis=-1)
    rows = jnp.concatenate([shares[:, None, :], kept_probs.astype(jnp.bfloat16)], axis=1)
    products = jnp.einsum(
        "rkb,rbc->rkc", rows, block_data[..., head_dim:], preferred_element_type=jnp.float32
    )
    merged_value = products[:, 0, :].astype(jnp.bfloat16).astype(jnp.float32)
    kept_weighted = products[:, 1:, :]
    merged_score = jnp.sum(shares.astype(jnp.float32)[:, None, :] * raw_qk, axis=-1)
    merged_score = merged_score + jnp.log(floored)[:, None]
    merged_score = jnp.where(has_merged[:, None], merged_score, -1e30)
    peaks = jnp.maximum(kept_peaks, merged_score)
    rescale = jnp.exp(kept_peaks - peaks)
    merged_prob = jnp.where(has_merged[:, None], jnp.exp(merged_score - peaks), 0.0)
    mass = kept_mass * rescale + merged_prob
    weighted = (
        kept_weighted * rescale[..., None]
        + merged_prob.astype(jnp.bfloat16).astype(jnp.float32)[..., None] * merged_value[:, None, :]
    )
    return (peaks, mass, weighted)


def route_tables(offsets, devices, capacity):
    requests = offsets.shape[0]
    index = jnp.arange(requests, dtype=jnp.int32)
    same = offsets[:, None] == offsets[None, :]
    position = jnp.sum((same & (index[None, :] < index[:, None])).astype(jnp.int32), axis=1)
    return position


def pack_slots(values, offsets, device, devices, capacity):
    requests = offsets.shape[0]
    index = jnp.arange(requests, dtype=jnp.int32)
    slot_ids = jnp.arange(devices * capacity, dtype=jnp.int32)
    amount = (slot_ids // capacity - device) % devices
    second = (slot_ids % capacity) == 1
    same = offsets[:, None] == offsets[None, :]
    earlier = jnp.sum((same & (index[None, :] < index[:, None])).astype(jnp.int32), axis=1)
    match = (
        (offsets[None, :] == amount[:, None])
        & (amount != 0)[:, None]
        & ((earlier[None, :] == 1) == second[:, None])
    )
    return jnp.dot(match.astype(values.dtype), values, precision=lax.Precision.HIGHEST)


def unpack_slots(received, values, offsets, position, device, devices, capacity):
    source = (device - offsets) % devices
    slots = source * capacity + jnp.minimum(position, capacity - 1)
    moving = offsets != 0
    flat = received.reshape(devices * capacity, -1)
    picks = (slots[:, None] == jnp.arange(devices * capacity, dtype=jnp.int32)[None, :]) & moving[:, None]
    taken = jnp.dot(picks.astype(values.dtype), flat, precision=lax.Precision.HIGHEST)
    return taken + jnp.where(moving[:, None], jnp.zeros((), values.dtype), values)


def join_partials(first, second):
    peak_one, mass_one, sum_one = first
    peak_two, mass_two, sum_two = second
    largest = jnp.maximum(peak_one, peak_two)
    scale_one = jnp.exp(peak_one - largest)
    scale_two = jnp.exp(peak_two - largest)
    return (
        largest,
        mass_one * scale_one + mass_two * scale_two,
        sum_one * scale_one[..., None] + sum_two * scale_two[..., None],
    )


def body(kv_cache, keep_lists, kept_counts, drop_scores, lengths, offsets, queries, out_weight):
    devices = lax.axis_size("kv")
    device = lax.axis_index("kv")
    requests, block_rows, width = kv_cache.shape
    head_dim = width // 2
    capacity = (requests // 2 + devices - 2) // (devices - 1)
    per_device = requests // devices
    codes = codes_for(keep_lists, kept_counts[:, 0], drop_scores, lengths, device)
    outgoing = pack_slots(codes, offsets, device, devices, capacity)
    received = lax.all_to_all(outgoing, "kv", split_axis=0, concat_axis=0, tiled=True)
    position = route_tables(offsets, devices, capacity)
    held_codes = unpack_slots(received, codes, offsets, position, device, devices, capacity)
    queries_h = queries.reshape(requests, -1, head_dim)
    heads = queries_h.shape[1]
    scores_qk = raw_scores(kv_cache, queries_h)
    peaks, mass, weighted = block_partial(kv_cache, held_codes, queries_h, scores_qk)
    stats = jnp.concatenate([peaks, mass], axis=1)
    stats = jnp.pad(stats, ((0, 0), (0, head_dim - 2 * heads)))
    payload = jnp.concatenate([weighted, stats[:, None, :]], axis=1)
    gathered = lax.all_to_all(payload, "kv", split_axis=0, concat_axis=0, tiled=True)
    gathered = gathered.reshape(devices, per_device, heads + 1, head_dim)
    sums = gathered[:, :, :heads, :]
    peaks_all = gathered[:, :, heads, :heads]
    mass_all = gathered[:, :, heads, heads : 2 * heads]
    largest = jnp.max(peaks_all, axis=0)
    factors = jnp.exp(peaks_all - largest[None])
    upper = jnp.sum(factors[..., None] * sums, axis=0)
    lower = jnp.sum(factors * mass_all, axis=0)
    attended = (upper / lower[..., None]).astype(jnp.bfloat16).reshape(per_device, -1)
    partial_out = jnp.dot(attended, out_weight, preferred_element_type=jnp.float32)
    groups = lax.axis_size("hd")
    pieces = partial_out.reshape(per_device, groups, -1).transpose(1, 0, 2)
    pieces = lax.all_to_all(pieces, "hd", split_axis=0, concat_axis=0, tiled=True)
    return jnp.sum(pieces, axis=0).astype(jnp.bfloat16)


def solution(mesh):
    in_specs = (
        P(None, "kv", None),
        P(None, "kv"),
        P(None, "kv"),
        P(None, "kv"),
        P(),
        P(),
        P(None, "hd"),
        P("hd", None),
    )
    out_specs = P("kv", "hd")
    return jax.shard_map(body, mesh=mesh, in_specs=in_specs, out_specs=out_specs, check_vma=False)
```

```python
import math

import jax
import jax.numpy as jnp
from jax import lax
from jax.sharding import PartitionSpec as P


def combined_all(value, axis, join):
    pieces = jax.tree.map(lambda part: lax.all_gather(part, axis), value)
    head = jax.tree.map(lambda part: part[0], pieces)
    tail = jax.tree.map(lambda part: part[1:], pieces)
    total, _ = lax.scan(lambda total, piece: (join(total, piece), None), head, tail)
    return total


def codes_for(keep_block, count_block, score_block, lengths, block_index):
    requests, block_rows = keep_block.shape
    low = 32
    high = block_rows // low
    places = jnp.arange(block_rows, dtype=jnp.int32)[None, :]
    counted_hi = jnp.where(places < count_block[:, None], keep_block >> 5, -1)
    upper = (counted_hi[..., None] == jnp.arange(high, dtype=jnp.int32)).astype(jnp.bfloat16)
    lower = ((keep_block & (low - 1))[..., None] == jnp.arange(low, dtype=jnp.int32)).astype(
        jnp.bfloat16
    )
    kept = jnp.einsum("rpa,rpb->rab", upper, lower, preferred_element_type=jnp.float32)
    kept_rows = kept.reshape(requests, block_rows) > 0.5
    position = block_index * block_rows + jnp.arange(block_rows, dtype=jnp.int32)
    valid_rows = position[None, :] < lengths[:, None]
    return jnp.where(valid_rows & kept_rows, -1.0, jnp.where(valid_rows, score_block, 0.0))


def raw_scores(block_data, queries_h):
    head_dim = queries_h.shape[-1]
    factor = 1.0 / math.sqrt(head_dim)
    scores_qk = jnp.einsum(
        "rhc,rbc->rhb",
        queries_h,
        block_data[..., :head_dim],
        preferred_element_type=jnp.float32,
    )
    return lax.optimization_barrier(scores_qk * factor)


def block_partial(block_data, codes, queries_h, scores_qk):
    head_dim = queries_h.shape[-1]
    kept_rows = codes < 0.0
    weight = jnp.maximum(codes, 0.0)
    totals = jnp.sum(weight, axis=1)
    has_merged = totals > 0.0
    floored = jnp.maximum(totals, 1.0)
    shares = (weight / floored[:, None]).astype(jnp.bfloat16)
    merged_score = jnp.sum(shares.astype(jnp.float32)[:, None, :] * scores_qk, axis=-1)
    merged_score = merged_score + jnp.log(floored)[:, None]
    merged_score = jnp.where(has_merged[:, None], merged_score, -1e30)
    scores_qk = jnp.where(kept_rows[:, None, :], scores_qk, -1e30)
    peaks = jnp.maximum(jnp.max(scores_qk, axis=-1), merged_score)
    probs = jnp.where(kept_rows[:, None, :], jnp.exp(scores_qk - peaks[..., None]), 0.0)
    merged_prob = jnp.where(has_merged[:, None], jnp.exp(merged_score - peaks), 0.0)
    mass = jnp.sum(probs, axis=-1) + merged_prob
    rows = jnp.concatenate([shares[:, None, :], probs.astype(jnp.bfloat16)], axis=1)
    products = jnp.einsum(
        "rkb,rbc->rkc", rows, block_data[..., head_dim:], preferred_element_type=jnp.float32
    )
    merged_value = products[:, 0, :].astype(jnp.bfloat16).astype(jnp.float32)
    weighted = (
        products[:, 1:, :]
        + merged_prob.astype(jnp.bfloat16).astype(jnp.float32)[..., None] * merged_value[:, None, :]
    )
    return (peaks, mass, weighted)


def route_tables(offsets, devices, capacity):
    requests = offsets.shape[0]
    index = jnp.arange(requests, dtype=jnp.int32)
    same = offsets[:, None] == offsets[None, :]
    position = jnp.sum((same & (index[None, :] < index[:, None])).astype(jnp.int32), axis=1)
    return position


def pack_slots(values, offsets, device, devices, capacity):
    requests = offsets.shape[0]
    index = jnp.arange(requests, dtype=jnp.int32)
    slot_ids = jnp.arange(devices * capacity, dtype=jnp.int32)
    amount = (slot_ids // capacity - device) % devices
    second = (slot_ids % capacity) == 1
    same = offsets[:, None] == offsets[None, :]
    earlier = jnp.sum((same & (index[None, :] < index[:, None])).astype(jnp.int32), axis=1)
    match = (
        (offsets[None, :] == amount[:, None])
        & (amount != 0)[:, None]
        & ((earlier[None, :] == 1) == second[:, None])
    )
    return jnp.dot(match.astype(values.dtype), values, precision=lax.Precision.HIGHEST)


def unpack_slots(received, values, offsets, position, device, devices, capacity):
    source = (device - offsets) % devices
    slots = source * capacity + jnp.minimum(position, capacity - 1)
    moving = offsets != 0
    flat = received.reshape(devices * capacity, -1)
    picks = (slots[:, None] == jnp.arange(devices * capacity, dtype=jnp.int32)[None, :]) & moving[:, None]
    taken = jnp.dot(picks.astype(values.dtype), flat, precision=lax.Precision.HIGHEST)
    return taken + jnp.where(moving[:, None], jnp.zeros((), values.dtype), values)


def join_partials(first, second):
    peak_one, mass_one, sum_one = first
    peak_two, mass_two, sum_two = second
    largest = jnp.maximum(peak_one, peak_two)
    scale_one = jnp.exp(peak_one - largest)
    scale_two = jnp.exp(peak_two - largest)
    return (
        largest,
        mass_one * scale_one + mass_two * scale_two,
        sum_one * scale_one[..., None] + sum_two * scale_two[..., None],
    )


def body(kv_cache, keep_lists, kept_counts, drop_scores, lengths, offsets, queries, out_weight):
    devices = lax.axis_size("kv")
    device = lax.axis_index("kv")
    requests, block_rows, width = kv_cache.shape
    head_dim = width // 2
    capacity = (requests // 2 + devices - 2) // (devices - 1)
    per_device = requests // devices
    codes = codes_for(keep_lists, kept_counts[:, 0], drop_scores, lengths, device)
    outgoing = pack_slots(codes, offsets, device, devices, capacity)
    received = lax.all_to_all(outgoing, "kv", split_axis=0, concat_axis=0, tiled=True)
    position = route_tables(offsets, devices, capacity)
    held_codes = unpack_slots(received, codes, offsets, position, device, devices, capacity)
    queries_h = queries.reshape(requests, -1, head_dim)
    heads = queries_h.shape[1]
    scores_qk = raw_scores(kv_cache, queries_h)
    peaks, mass, weighted = block_partial(kv_cache, held_codes, queries_h, scores_qk)
    stats = jnp.concatenate([peaks, mass], axis=1)
    stats = jnp.pad(stats, ((0, 0), (0, head_dim - 2 * heads)))
    payload = jnp.concatenate([weighted, stats[:, None, :]], axis=1)
    gathered = lax.all_to_all(payload, "kv", split_axis=0, concat_axis=0, tiled=True)
    gathered = gathered.reshape(devices, per_device, heads + 1, head_dim)
    sums = gathered[:, :, :heads, :]
    peaks_all = gathered[:, :, heads, :heads]
    mass_all = gathered[:, :, heads, heads : 2 * heads]
    largest = jnp.max(peaks_all, axis=0)
    factors = jnp.exp(peaks_all - largest[None])
    upper = jnp.sum(factors[..., None] * sums, axis=0)
    lower = jnp.sum(factors * mass_all, axis=0)
    attended = (upper / lower[..., None]).astype(jnp.bfloat16).reshape(per_device, -1)
    partial_out = jnp.dot(attended, out_weight, preferred_element_type=jnp.float32)
    groups = lax.axis_size("hd")
    pieces = partial_out.reshape(per_device, groups, -1).transpose(1, 0, 2)
    pieces = lax.all_to_all(pieces, "hd", split_axis=0, concat_axis=0, tiled=True)
    return jnp.sum(pieces, axis=0).astype(jnp.bfloat16)


def solution(mesh):
    in_specs = (
        P(None, "kv", None),
        P(None, "kv"),
        P(None, "kv"),
        P(None, "kv"),
        P(),
        P(),
        P(None, "hd"),
        P("hd", None),
    )
    out_specs = P("kv", "hd")
    return jax.shard_map(body, mesh=mesh, in_specs=in_specs, out_specs=out_specs, check_vma=False)
```

```python
import math

import jax
import jax.numpy as jnp
from jax import lax
from jax.sharding import PartitionSpec as P


def combined_all(value, axis, join):
    pieces = jax.tree.map(lambda part: lax.all_gather(part, axis), value)
    head = jax.tree.map(lambda part: part[0], pieces)
    tail = jax.tree.map(lambda part: part[1:], pieces)
    total, _ = lax.scan(lambda total, piece: (join(total, piece), None), head, tail)
    return total


def codes_for(keep_block, count_block, score_block, lengths, block_index):
    requests, block_rows = keep_block.shape
    low = 32
    high = block_rows // low
    places = jnp.arange(block_rows, dtype=jnp.int32)[None, :]
    counted_hi = jnp.where(places < count_block[:, None], keep_block >> 5, -1)
    upper = (counted_hi[..., None] == jnp.arange(high, dtype=jnp.int32)).astype(jnp.bfloat16)
    lower = ((keep_block & (low - 1))[..., None] == jnp.arange(low, dtype=jnp.int32)).astype(
        jnp.bfloat16
    )
    kept = jnp.einsum("rpa,rpb->rab", upper, lower, preferred_element_type=jnp.float32)
    kept_rows = kept.reshape(requests, block_rows) > 0.5
    position = block_index * block_rows + jnp.arange(block_rows, dtype=jnp.int32)
    valid_rows = position[None, :] < lengths[:, None]
    return jnp.where(valid_rows & kept_rows, -1.0, jnp.where(valid_rows, score_block, 0.0))


def raw_scores(block_data, queries_h):
    head_dim = queries_h.shape[-1]
    factor = 1.0 / math.sqrt(head_dim)
    scores_qk = jnp.einsum(
        "rhc,rbc->rhb",
        queries_h,
        block_data[..., :head_dim],
        preferred_element_type=jnp.float32,
    )
    return lax.optimization_barrier(scores_qk * factor)


def block_partial(block_data, codes, queries_h, scores_qk):
    head_dim = queries_h.shape[-1]
    kept_rows = codes < 0.0
    weight = jnp.maximum(codes, 0.0)
    totals = jnp.sum(weight, axis=1)
    has_merged = totals > 0.0
    floored = jnp.maximum(totals, 1.0)
    shares = (weight / floored[:, None]).astype(jnp.bfloat16)
    merged_score = jnp.sum(shares.astype(jnp.float32)[:, None, :] * scores_qk, axis=-1)
    merged_score = merged_score + jnp.log(floored)[:, None]
    merged_score = jnp.where(has_merged[:, None], merged_score, -1e30)
    scores_qk = jnp.where(kept_rows[:, None, :], scores_qk, -1e30)
    peaks = jnp.maximum(jnp.max(scores_qk, axis=-1), merged_score)
    probs = jnp.where(kept_rows[:, None, :], jnp.exp(scores_qk - peaks[..., None]), 0.0)
    merged_prob = jnp.where(has_merged[:, None], jnp.exp(merged_score - peaks), 0.0)
    mass = jnp.sum(probs, axis=-1) + merged_prob
    rows = jnp.concatenate([shares[:, None, :], probs.astype(jnp.bfloat16)], axis=1)
    products = jnp.einsum(
        "rkb,rbc->rkc", rows, block_data[..., head_dim:], preferred_element_type=jnp.float32
    )
    merged_value = products[:, 0, :].astype(jnp.bfloat16).astype(jnp.float32)
    weighted = (
        products[:, 1:, :]
        + merged_prob.astype(jnp.bfloat16).astype(jnp.float32)[..., None] * merged_value[:, None, :]
    )
    return (peaks, mass, weighted)


def route_tables(offsets, devices, capacity):
    requests = offsets.shape[0]
    index = jnp.arange(requests, dtype=jnp.int32)
    same = offsets[:, None] == offsets[None, :]
    position = jnp.sum((same & (index[None, :] < index[:, None])).astype(jnp.int32), axis=1)
    return position


def pack_slots(values, offsets, device, devices, capacity):
    requests = offsets.shape[0]
    index = jnp.arange(requests, dtype=jnp.int32)
    slot_ids = jnp.arange(devices * capacity, dtype=jnp.int32)
    amount = (slot_ids // capacity - device) % devices
    second = (slot_ids % capacity) == 1
    same = offsets[:, None] == offsets[None, :]
    earlier = jnp.sum((same & (index[None, :] < index[:, None])).astype(jnp.int32), axis=1)
    match = (
        (offsets[None, :] == amount[:, None])
        & (amount != 0)[:, None]
        & ((earlier[None, :] == 1) == second[:, None])
    )
    return jnp.dot(match.astype(values.dtype), values, precision=lax.Precision.HIGHEST)


def unpack_slots(received, values, offsets, position, device, devices, capacity):
    source = (device - offsets) % devices
    slots = source * capacity + jnp.minimum(position, capacity - 1)
    moving = offsets != 0
    flat = received.reshape(devices * capacity, -1)
    picks = (slots[:, None] == jnp.arange(devices * capacity, dtype=jnp.int32)[None, :]) & moving[:, None]
    taken = jnp.dot(picks.astype(values.dtype), flat, precision=lax.Precision.HIGHEST)
    return taken + jnp.where(moving[:, None], jnp.zeros((), values.dtype), values)


def join_partials(first, second):
    peak_one, mass_one, sum_one = first
    peak_two, mass_two, sum_two = second
    largest = jnp.maximum(peak_one, peak_two)
    scale_one = jnp.exp(peak_one - largest)
    scale_two = jnp.exp(peak_two - largest)
    return (
        largest,
        mass_one * scale_one + mass_two * scale_two,
        sum_one * scale_one[..., None] + sum_two * scale_two[..., None],
    )


def body(kv_cache, keep_lists, kept_counts, drop_scores, lengths, offsets, queries, out_weight):
    devices = lax.axis_size("kv")
    device = lax.axis_index("kv")
    requests, block_rows, width = kv_cache.shape
    head_dim = width // 2
    capacity = (requests // 2 + devices - 2) // (devices - 1)
    per_device = requests // devices
    codes = codes_for(keep_lists, kept_counts[:, 0], drop_scores, lengths, device)
    outgoing = pack_slots(codes, offsets, device, devices, capacity)
    received = lax.all_to_all(outgoing, "kv", split_axis=0, concat_axis=0, tiled=True)
    position = route_tables(offsets, devices, capacity)
    held_codes = unpack_slots(received, codes, offsets, position, device, devices, capacity)
    queries_h = queries.reshape(requests, -1, head_dim)
    heads = queries_h.shape[1]
    scores_qk = raw_scores(kv_cache, queries_h)
    peaks, mass, weighted = block_partial(kv_cache, held_codes, queries_h, scores_qk)
    stats = jnp.concatenate([peaks, mass], axis=1)
    stats = jnp.pad(stats, ((0, 0), (0, head_dim - 2 * heads)))
    payload = jnp.concatenate([weighted, stats[:, None, :]], axis=1)
    gathered = lax.all_to_all(payload, "kv", split_axis=0, concat_axis=0, tiled=True)
    gathered = gathered.reshape(devices, per_device, heads + 1, head_dim)
    sums = gathered[:, :, :heads, :]
    peaks_all = gathered[:, :, heads, :heads]
    mass_all = gathered[:, :, heads, heads : 2 * heads]
    largest = jnp.max(peaks_all, axis=0)
    factors = jnp.exp(peaks_all - largest[None])
    upper = jnp.sum(factors[..., None] * sums, axis=0)
    lower = jnp.sum(factors * mass_all, axis=0)
    attended = (upper / lower[..., None]).astype(jnp.bfloat16).reshape(per_device, -1)
    partial_out = jnp.dot(attended, out_weight, preferred_element_type=jnp.float32)
    groups = lax.axis_size("hd")
    group = lax.axis_index("hd")
    pieces = partial_out.reshape(per_device, groups, -1).transpose(1, 0, 2)
    total = lax.dynamic_index_in_dim(pieces, group, 0, keepdims=False)
    for shift in range(1, groups):
        target = (group + shift) % groups
        piece = lax.dynamic_index_in_dim(pieces, target, 0, keepdims=False)
        pairs = [(i, (i + shift) % groups) for i in range(groups)]
        total = total + lax.ppermute(piece, "hd", pairs)
    return total.astype(jnp.bfloat16)


def solution(mesh):
    in_specs = (
        P(None, "kv", None),
        P(None, "kv"),
        P(None, "kv"),
        P(None, "kv"),
        P(),
        P(),
        P(None, "hd"),
        P("hd", None),
    )
    out_specs = P("kv", "hd")
    return jax.shard_map(body, mesh=mesh, in_specs=in_specs, out_specs=out_specs, check_vma=False)
```

```python
import math

import jax
import jax.numpy as jnp
from jax import lax
from jax.sharding import PartitionSpec as P


def combined_all(value, axis, join):
    pieces = jax.tree.map(lambda part: lax.all_gather(part, axis), value)
    head = jax.tree.map(lambda part: part[0], pieces)
    tail = jax.tree.map(lambda part: part[1:], pieces)
    total, _ = lax.scan(lambda total, piece: (join(total, piece), None), head, tail)
    return total


def codes_for(keep_block, count_block, score_block, lengths, block_index):
    requests, block_rows = keep_block.shape
    low = 32
    high = block_rows // low
    places = jnp.arange(block_rows, dtype=jnp.int32)[None, :]
    counted_hi = jnp.where(places < count_block[:, None], keep_block >> 5, -1)
    upper = (counted_hi[..., None] == jnp.arange(high, dtype=jnp.int32)).astype(jnp.bfloat16)
    lower = ((keep_block & (low - 1))[..., None] == jnp.arange(low, dtype=jnp.int32)).astype(
        jnp.bfloat16
    )
    kept = jnp.einsum("rpa,rpb->rab", upper, lower, preferred_element_type=jnp.float32)
    kept_rows = kept.reshape(requests, block_rows) > 0.5
    position = block_index * block_rows + jnp.arange(block_rows, dtype=jnp.int32)
    valid_rows = position[None, :] < lengths[:, None]
    return jnp.where(valid_rows & kept_rows, -1.0, jnp.where(valid_rows, score_block, 0.0))


def raw_scores(block_data, queries_h):
    head_dim = queries_h.shape[-1]
    factor = 1.0 / math.sqrt(head_dim)
    scores_qk = jnp.einsum(
        "rhc,rbc->rhb",
        queries_h,
        block_data[..., :head_dim],
        preferred_element_type=jnp.float32,
    )
    return lax.optimization_barrier(scores_qk * factor)


def block_partial(block_data, codes, queries_h, scores_qk):
    head_dim = queries_h.shape[-1]
    kept_rows = codes < 0.0
    weight = jnp.maximum(codes, 0.0)
    totals = jnp.sum(weight, axis=1)
    has_merged = totals > 0.0
    floored = jnp.maximum(totals, 1.0)
    shares = (weight / floored[:, None]).astype(jnp.bfloat16)
    merged_score = jnp.sum(shares.astype(jnp.float32)[:, None, :] * scores_qk, axis=-1)
    merged_score = merged_score + jnp.log(floored)[:, None]
    merged_score = jnp.where(has_merged[:, None], merged_score, -1e30)
    scores_qk = jnp.where(kept_rows[:, None, :], scores_qk, -1e30)
    peaks = jnp.maximum(jnp.max(scores_qk, axis=-1), merged_score)
    probs = jnp.where(kept_rows[:, None, :], jnp.exp(scores_qk - peaks[..., None]), 0.0)
    merged_prob = jnp.where(has_merged[:, None], jnp.exp(merged_score - peaks), 0.0)
    mass = jnp.sum(probs, axis=-1) + merged_prob
    rows = jnp.concatenate([shares[:, None, :], probs.astype(jnp.bfloat16)], axis=1)
    products = jnp.einsum(
        "rkb,rbc->rkc", rows, block_data[..., head_dim:], preferred_element_type=jnp.float32
    )
    merged_value = products[:, 0, :].astype(jnp.bfloat16).astype(jnp.float32)
    weighted = (
        products[:, 1:, :]
        + merged_prob.astype(jnp.bfloat16).astype(jnp.float32)[..., None] * merged_value[:, None, :]
    )
    return (peaks, mass, weighted)


def route_tables(offsets, devices, capacity):
    requests = offsets.shape[0]
    index = jnp.arange(requests, dtype=jnp.int32)
    same = offsets[:, None] == offsets[None, :]
    position = jnp.sum((same & (index[None, :] < index[:, None])).astype(jnp.int32), axis=1)
    return position


def pack_slots(values, offsets, device, devices, capacity):
    requests = offsets.shape[0]
    index = jnp.arange(requests, dtype=jnp.int32)
    slot_ids = jnp.arange(devices * capacity, dtype=jnp.int32)
    amount = (slot_ids // capacity - device) % devices
    second = (slot_ids % capacity) == 1
    same = offsets[:, None] == offsets[None, :]
    earlier = jnp.sum((same & (index[None, :] < index[:, None])).astype(jnp.int32), axis=1)
    match = (
        (offsets[None, :] == amount[:, None])
        & (amount != 0)[:, None]
        & ((earlier[None, :] == 1) == second[:, None])
    )
    return jnp.dot(match.astype(values.dtype), values, precision=lax.Precision.HIGHEST)


def unpack_slots(received, values, offsets, position, device, devices, capacity):
    source = (device - offsets) % devices
    slots = source * capacity + jnp.minimum(position, capacity - 1)
    moving = offsets != 0
    flat = received.reshape(devices * capacity, -1)
    picks = (slots[:, None] == jnp.arange(devices * capacity, dtype=jnp.int32)[None, :]) & moving[:, None]
    taken = jnp.dot(picks.astype(values.dtype), flat, precision=lax.Precision.HIGHEST)
    return taken + jnp.where(moving[:, None], jnp.zeros((), values.dtype), values)


def join_partials(first, second):
    peak_one, mass_one, sum_one = first
    peak_two, mass_two, sum_two = second
    largest = jnp.maximum(peak_one, peak_two)
    scale_one = jnp.exp(peak_one - largest)
    scale_two = jnp.exp(peak_two - largest)
    return (
        largest,
        mass_one * scale_one + mass_two * scale_two,
        sum_one * scale_one[..., None] + sum_two * scale_two[..., None],
    )


def body(kv_cache, keep_lists, kept_counts, drop_scores, lengths, offsets, queries, out_weight):
    devices = lax.axis_size("kv")
    device = lax.axis_index("kv")
    requests, block_rows, width = kv_cache.shape
    head_dim = width // 2
    capacity = (requests // 2 + devices - 2) // (devices - 1)
    per_device = requests // devices
    codes = codes_for(keep_lists, kept_counts[:, 0], drop_scores, lengths, device)
    outgoing = pack_slots(codes, offsets, device, devices, capacity)
    received = lax.all_to_all(outgoing, "kv", split_axis=0, concat_axis=0, tiled=True)
    position = route_tables(offsets, devices, capacity)
    held_codes = unpack_slots(received, codes, offsets, position, device, devices, capacity)
    queries_h = queries.reshape(requests, -1, head_dim)
    heads = queries_h.shape[1]
    scores_qk = raw_scores(kv_cache, queries_h)
    peaks, mass, weighted = block_partial(kv_cache, held_codes, queries_h, scores_qk)
    stats = jnp.concatenate([peaks, mass], axis=1)
    stats = jnp.pad(stats, ((0, 0), (0, head_dim - 2 * heads)))
    payload = jnp.concatenate([weighted, stats[:, None, :]], axis=1)
    gathered = lax.all_to_all(payload, "kv", split_axis=0, concat_axis=0, tiled=True)
    gathered = gathered.reshape(devices, per_device, heads + 1, head_dim)
    sums = gathered[:, :, :heads, :]
    peaks_all = gathered[:, :, heads, :heads]
    mass_all = gathered[:, :, heads, heads : 2 * heads]
    largest = jnp.max(peaks_all, axis=0)
    factors = jnp.exp(peaks_all - largest[None])
    upper = jnp.sum(factors[..., None] * sums, axis=0)
    lower = jnp.sum(factors * mass_all, axis=0)
    attended = (upper / lower[..., None]).astype(jnp.bfloat16).reshape(per_device, -1)
    partial_out = jnp.dot(attended, out_weight, preferred_element_type=jnp.float32)
    groups = lax.axis_size("hd")
    group = lax.axis_index("hd")
    pieces = partial_out.reshape(per_device, groups, -1).transpose(1, 0, 2)
    return halving_sum(pieces, group, groups, "hd").astype(jnp.bfloat16)


def halving_sum(pieces, group, groups, axis):
    if groups & (groups - 1):
        total = lax.dynamic_index_in_dim(pieces, group, 0, keepdims=False)
        for shift in range(1, groups):
            piece = lax.dynamic_index_in_dim(pieces, (group + shift) % groups, 0, keepdims=False)
            pairs = [(i, (i + shift) % groups) for i in range(groups)]
            total = total + lax.ppermute(piece, axis, pairs)
        return total
    width = groups
    while width > 1:
        width //= 2
        pairs = [(i, i ^ width) for i in range(groups)]
        own = (group & width) // width
        keep = lax.dynamic_slice_in_dim(pieces, own * width, width, 0)
        send = lax.dynamic_slice_in_dim(pieces, (1 - own) * width, width, 0)
        pieces = keep + lax.ppermute(send, axis, pairs)
    return pieces[0]


def solution(mesh):
    in_specs = (
        P(None, "kv", None),
        P(None, "kv"),
        P(None, "kv"),
        P(None, "kv"),
        P(),
        P(),
        P(None, "hd"),
        P("hd", None),
    )
    out_specs = P("kv", "hd")
    return jax.shard_map(body, mesh=mesh, in_specs=in_specs, out_specs=out_specs, check_vma=False)
```

```python
import math

import jax
import jax.numpy as jnp
from jax import lax
from jax.sharding import PartitionSpec as P


def combined_all(value, axis, join):
    pieces = jax.tree.map(lambda part: lax.all_gather(part, axis), value)
    head = jax.tree.map(lambda part: part[0], pieces)
    tail = jax.tree.map(lambda part: part[1:], pieces)
    total, _ = lax.scan(lambda total, piece: (join(total, piece), None), head, tail)
    return total


def codes_for(keep_block, count_block, score_block, lengths, block_index):
    requests, block_rows = keep_block.shape
    low = 32
    high = block_rows // low
    places = jnp.arange(block_rows, dtype=jnp.int32)[None, :]
    counted_hi = jnp.where(places < count_block[:, None], keep_block >> 5, -1)
    upper = (counted_hi[..., None] == jnp.arange(high, dtype=jnp.int32)).astype(jnp.bfloat16)
    lower = ((keep_block & (low - 1))[..., None] == jnp.arange(low, dtype=jnp.int32)).astype(
        jnp.bfloat16
    )
    kept = jnp.einsum("rpa,rpb->rab", upper, lower, preferred_element_type=jnp.float32)
    kept_rows = kept.reshape(requests, block_rows) > 0.5
    position = block_index * block_rows + jnp.arange(block_rows, dtype=jnp.int32)
    valid_rows = position[None, :] < lengths[:, None]
    return jnp.where(valid_rows & kept_rows, -1.0, jnp.where(valid_rows, score_block, 0.0))


def raw_scores(block_data, queries_h):
    head_dim = queries_h.shape[-1]
    factor = 1.0 / math.sqrt(head_dim)
    scores_qk = jnp.einsum(
        "rhc,rbc->rhb",
        queries_h,
        block_data[..., :head_dim],
        preferred_element_type=jnp.float32,
    )
    return lax.optimization_barrier(scores_qk * factor)


def block_partial(block_data, codes, queries_h, scores_qk):
    head_dim = queries_h.shape[-1]
    kept_rows = codes < 0.0
    weight = jnp.maximum(codes, 0.0)
    totals = jnp.sum(weight, axis=1)
    has_merged = totals > 0.0
    floored = jnp.maximum(totals, 1.0)
    shares = (weight / floored[:, None]).astype(jnp.bfloat16)
    merged_score = jnp.sum(shares.astype(jnp.float32)[:, None, :] * scores_qk, axis=-1)
    merged_score = merged_score + jnp.log(floored)[:, None]
    merged_score = jnp.where(has_merged[:, None], merged_score, -1e30)
    scores_qk = jnp.where(kept_rows[:, None, :], scores_qk, -1e30)
    peaks = jnp.maximum(jnp.max(scores_qk, axis=-1), merged_score)
    probs = jnp.where(kept_rows[:, None, :], jnp.exp(scores_qk - peaks[..., None]), 0.0)
    merged_prob = jnp.where(has_merged[:, None], jnp.exp(merged_score - peaks), 0.0)
    mass = jnp.sum(probs, axis=-1) + merged_prob
    rows = jnp.concatenate([shares[:, None, :], probs.astype(jnp.bfloat16)], axis=1)
    products = jnp.einsum(
        "rkb,rbc->rkc", rows, block_data[..., head_dim:], preferred_element_type=jnp.float32
    )
    merged_value = products[:, 0, :].astype(jnp.bfloat16).astype(jnp.float32)
    weighted = (
        products[:, 1:, :]
        + merged_prob.astype(jnp.bfloat16).astype(jnp.float32)[..., None] * merged_value[:, None, :]
    )
    return (peaks, mass, weighted)


def route_tables(offsets, devices, capacity):
    requests = offsets.shape[0]
    index = jnp.arange(requests, dtype=jnp.int32)
    same = offsets[:, None] == offsets[None, :]
    position = jnp.sum((same & (index[None, :] < index[:, None])).astype(jnp.int32), axis=1)
    return position


def pack_slots(values, offsets, device, devices, capacity):
    requests = offsets.shape[0]
    index = jnp.arange(requests, dtype=jnp.int32)
    slot_ids = jnp.arange(devices * capacity, dtype=jnp.int32)
    amount = (slot_ids // capacity - device) % devices
    second = (slot_ids % capacity) == 1
    same = offsets[:, None] == offsets[None, :]
    earlier = jnp.sum((same & (index[None, :] < index[:, None])).astype(jnp.int32), axis=1)
    match = (
        (offsets[None, :] == amount[:, None])
        & (amount != 0)[:, None]
        & ((earlier[None, :] == 1) == second[:, None])
    )
    return jnp.dot(match.astype(values.dtype), values, precision=lax.Precision.HIGHEST)


def unpack_slots(received, values, offsets, position, device, devices, capacity):
    source = (device - offsets) % devices
    slots = source * capacity + jnp.minimum(position, capacity - 1)
    moving = offsets != 0
    flat = received.reshape(devices * capacity, -1)
    picks = (slots[:, None] == jnp.arange(devices * capacity, dtype=jnp.int32)[None, :]) & moving[:, None]
    taken = jnp.dot(picks.astype(values.dtype), flat, precision=lax.Precision.HIGHEST)
    return taken + jnp.where(moving[:, None], jnp.zeros((), values.dtype), values)


def join_partials(first, second):
    peak_one, mass_one, sum_one = first
    peak_two, mass_two, sum_two = second
    largest = jnp.maximum(peak_one, peak_two)
    scale_one = jnp.exp(peak_one - largest)
    scale_two = jnp.exp(peak_two - largest)
    return (
        largest,
        mass_one * scale_one + mass_two * scale_two,
        sum_one * scale_one[..., None] + sum_two * scale_two[..., None],
    )


def body(kv_cache, keep_lists, kept_counts, drop_scores, lengths, offsets, queries, out_weight):
    devices = lax.axis_size("kv")
    device = lax.axis_index("kv")
    requests, block_rows, width = kv_cache.shape
    head_dim = width // 2
    capacity = (requests // 2 + devices - 2) // (devices - 1)
    per_device = requests // devices
    codes = codes_for(keep_lists, kept_counts[:, 0], drop_scores, lengths, device)
    outgoing = pack_slots(codes, offsets, device, devices, capacity)
    received = lax.all_to_all(outgoing, "kv", split_axis=0, concat_axis=0, tiled=True)
    position = route_tables(offsets, devices, capacity)
    held_codes = unpack_slots(received, codes, offsets, position, device, devices, capacity)
    queries_h = queries.reshape(requests, -1, head_dim)
    heads = queries_h.shape[1]
    scores_qk = raw_scores(kv_cache, queries_h)
    peaks, mass, weighted = block_partial(kv_cache, held_codes, queries_h, scores_qk)
    stats = jnp.concatenate([peaks, mass], axis=1)
    stats = jnp.pad(stats, ((0, 0), (0, head_dim - 2 * heads)))
    payload = jnp.concatenate([weighted, stats[:, None, :]], axis=1)
    gathered = lax.all_to_all(payload, "kv", split_axis=0, concat_axis=0, tiled=True)
    gathered = gathered.reshape(devices, per_device, heads + 1, head_dim)
    sums = gathered[:, :, :heads, :]
    peaks_all = gathered[:, :, heads, :heads]
    mass_all = gathered[:, :, heads, heads : 2 * heads]
    largest = jnp.max(peaks_all, axis=0)
    factors = jnp.exp(peaks_all - largest[None])
    upper = jnp.sum(factors[..., None] * sums, axis=0)
    lower = jnp.sum(factors * mass_all, axis=0)
    attended = (upper / lower[..., None]).astype(jnp.bfloat16).reshape(per_device, -1)
    partial_out = jnp.dot(attended, out_weight, preferred_element_type=jnp.float32)
    groups = lax.axis_size("hd")
    group = lax.axis_index("hd")
    pieces = partial_out.reshape(per_device, groups, -1).transpose(1, 0, 2)
    total = lax.dynamic_index_in_dim(pieces, group, 0, keepdims=False)
    for shift in sorted(range(1, groups), key=lambda s: -min(s, groups - s)):
        target = (group + shift) % groups
        piece = lax.dynamic_index_in_dim(pieces, target, 0, keepdims=False)
        pairs = [(i, (i + shift) % groups) for i in range(groups)]
        total = total + lax.ppermute(piece, "hd", pairs)
    return total.astype(jnp.bfloat16)


def solution(mesh):
    in_specs = (
        P(None, "kv", None),
        P(None, "kv"),
        P(None, "kv"),
        P(None, "kv"),
        P(),
        P(),
        P(None, "hd"),
        P("hd", None),
    )
    out_specs = P("kv", "hd")
    return jax.shard_map(body, mesh=mesh, in_specs=in_specs, out_specs=out_specs, check_vma=False)
```

```python
import math

import jax
import jax.numpy as jnp
from jax import lax
from jax.sharding import PartitionSpec as P


def combined_all(value, axis, join):
    pieces = jax.tree.map(lambda part: lax.all_gather(part, axis), value)
    head = jax.tree.map(lambda part: part[0], pieces)
    tail = jax.tree.map(lambda part: part[1:], pieces)
    total, _ = lax.scan(lambda total, piece: (join(total, piece), None), head, tail)
    return total


def codes_for(keep_block, count_block, score_block, lengths, block_index):
    requests, block_rows = keep_block.shape
    low = 32
    high = block_rows // low
    places = jnp.arange(block_rows, dtype=jnp.int32)[None, :]
    counted_hi = jnp.where(places < count_block[:, None], keep_block >> 5, -1)
    upper = (counted_hi[..., None] == jnp.arange(high, dtype=jnp.int32)).astype(jnp.bfloat16)
    lower = ((keep_block & (low - 1))[..., None] == jnp.arange(low, dtype=jnp.int32)).astype(
        jnp.bfloat16
    )
    kept = jnp.einsum("rpa,rpb->rab", upper, lower, preferred_element_type=jnp.float32)
    kept_rows = kept.reshape(requests, block_rows) > 0.5
    position = block_index * block_rows + jnp.arange(block_rows, dtype=jnp.int32)
    valid_rows = position[None, :] < lengths[:, None]
    return jnp.where(valid_rows & kept_rows, -1.0, jnp.where(valid_rows, score_block, 0.0))


def raw_scores(block_data, queries_h):
    head_dim = queries_h.shape[-1]
    factor = 1.0 / math.sqrt(head_dim)
    scores_qk = jnp.einsum(
        "rhc,rbc->rhb",
        queries_h,
        block_data[..., :head_dim],
        preferred_element_type=jnp.float32,
    )
    return lax.optimization_barrier(scores_qk * factor)


def block_partial(block_data, codes, queries_h, scores_qk):
    head_dim = queries_h.shape[-1]
    kept_rows = codes < 0.0
    weight = jnp.maximum(codes, 0.0)
    totals = jnp.sum(weight, axis=1)
    has_merged = totals > 0.0
    floored = jnp.maximum(totals, 1.0)
    shares = (weight / floored[:, None]).astype(jnp.bfloat16)
    merged_score = jnp.sum(shares.astype(jnp.float32)[:, None, :] * scores_qk, axis=-1)
    merged_score = merged_score + jnp.log(floored)[:, None]
    merged_score = jnp.where(has_merged[:, None], merged_score, -1e30)
    scores_qk = jnp.where(kept_rows[:, None, :], scores_qk, -1e30)
    peaks = jnp.maximum(jnp.max(scores_qk, axis=-1), merged_score)
    probs = jnp.where(kept_rows[:, None, :], jnp.exp(scores_qk - peaks[..., None]), 0.0)
    merged_prob = jnp.where(has_merged[:, None], jnp.exp(merged_score - peaks), 0.0)
    mass = jnp.sum(probs, axis=-1) + merged_prob
    rows = jnp.concatenate([shares[:, None, :], probs.astype(jnp.bfloat16)], axis=1)
    products = jnp.einsum(
        "rkb,rbc->rkc", rows, block_data[..., head_dim:], preferred_element_type=jnp.float32
    )
    merged_value = products[:, 0, :].astype(jnp.bfloat16).astype(jnp.float32)
    weighted = (
        products[:, 1:, :]
        + merged_prob.astype(jnp.bfloat16).astype(jnp.float32)[..., None] * merged_value[:, None, :]
    )
    return (peaks, mass, weighted)


def route_tables(offsets, devices, capacity):
    requests = offsets.shape[0]
    index = jnp.arange(requests, dtype=jnp.int32)
    same = offsets[:, None] == offsets[None, :]
    position = jnp.sum((same & (index[None, :] < index[:, None])).astype(jnp.int32), axis=1)
    return position


def pack_slots(values, offsets, device, devices, capacity):
    requests = offsets.shape[0]
    depth = 8
    index = jnp.arange(requests, dtype=jnp.int32)
    slot_ids = jnp.arange(devices * depth, dtype=jnp.int32)
    amount = (slot_ids // depth - device) % devices
    slot = slot_ids % depth
    same = offsets[:, None] == offsets[None, :]
    earlier = jnp.sum((same & (index[None, :] < index[:, None])).astype(jnp.int32), axis=1)
    match = (
        (offsets[None, :] == amount[:, None])
        & ((amount != 0) & (slot < capacity))[:, None]
        & (earlier[None, :] == slot[:, None])
    )
    sent = jnp.dot(match.astype(values.dtype), values, precision=lax.Precision.HIGHEST)
    return sent.reshape(devices, depth, -1)


def unpack_slots(received, values, offsets, position, device, devices, capacity):
    source = (device - offsets) % devices
    depth = received.shape[1]
    slots = source * depth + jnp.minimum(position, capacity - 1)
    moving = offsets != 0
    flat = received.reshape(devices * depth, -1)
    picks = (slots[:, None] == jnp.arange(devices * depth, dtype=jnp.int32)[None, :]) & moving[:, None]
    taken = jnp.dot(picks.astype(values.dtype), flat, precision=lax.Precision.HIGHEST)
    return taken + jnp.where(moving[:, None], jnp.zeros((), values.dtype), values)


def join_partials(first, second):
    peak_one, mass_one, sum_one = first
    peak_two, mass_two, sum_two = second
    largest = jnp.maximum(peak_one, peak_two)
    scale_one = jnp.exp(peak_one - largest)
    scale_two = jnp.exp(peak_two - largest)
    return (
        largest,
        mass_one * scale_one + mass_two * scale_two,
        sum_one * scale_one[..., None] + sum_two * scale_two[..., None],
    )


def body(kv_cache, keep_lists, kept_counts, drop_scores, lengths, offsets, queries, out_weight):
    devices = lax.axis_size("kv")
    device = lax.axis_index("kv")
    requests, block_rows, width = kv_cache.shape
    head_dim = width // 2
    capacity = (requests // 2 + devices - 2) // (devices - 1)
    per_device = requests // devices
    codes = codes_for(keep_lists, kept_counts[:, 0], drop_scores, lengths, device)
    outgoing = pack_slots(codes, offsets, device, devices, capacity)
    received = lax.all_to_all(outgoing, "kv", split_axis=0, concat_axis=0, tiled=True)
    position = route_tables(offsets, devices, capacity)
    held_codes = unpack_slots(received, codes, offsets, position, device, devices, capacity)
    queries_h = queries.reshape(requests, -1, head_dim)
    heads = queries_h.shape[1]
    scores_qk = raw_scores(kv_cache, queries_h)
    peaks, mass, weighted = block_partial(kv_cache, held_codes, queries_h, scores_qk)
    stats = jnp.concatenate([peaks, mass], axis=1)
    stats = jnp.pad(stats, ((0, 0), (0, head_dim - 2 * heads)))
    payload = jnp.concatenate([weighted, stats[:, None, :]], axis=1)
    gathered = lax.all_to_all(payload, "kv", split_axis=0, concat_axis=0, tiled=True)
    gathered = gathered.reshape(devices, per_device, heads + 1, head_dim)
    sums = gathered[:, :, :heads, :]
    peaks_all = gathered[:, :, heads, :heads]
    mass_all = gathered[:, :, heads, heads : 2 * heads]
    largest = jnp.max(peaks_all, axis=0)
    factors = jnp.exp(peaks_all - largest[None])
    upper = jnp.sum(factors[..., None] * sums, axis=0)
    lower = jnp.sum(factors * mass_all, axis=0)
    attended = (upper / lower[..., None]).astype(jnp.bfloat16).reshape(per_device, -1)
    partial_out = jnp.dot(attended, out_weight, preferred_element_type=jnp.float32)
    groups = lax.axis_size("hd")
    group = lax.axis_index("hd")
    pieces = partial_out.reshape(per_device, groups, -1).transpose(1, 0, 2)
    total = lax.dynamic_index_in_dim(pieces, group, 0, keepdims=False)
    for shift in range(1, groups):
        target = (group + shift) % groups
        piece = lax.dynamic_index_in_dim(pieces, target, 0, keepdims=False)
        pairs = [(i, (i + shift) % groups) for i in range(groups)]
        total = total + lax.ppermute(piece, "hd", pairs)
    return total.astype(jnp.bfloat16)


def solution(mesh):
    in_specs = (
        P(None, "kv", None),
        P(None, "kv"),
        P(None, "kv"),
        P(None, "kv"),
        P(),
        P(),
        P(None, "hd"),
        P("hd", None),
    )
    out_specs = P("kv", "hd")
    return jax.shard_map(body, mesh=mesh, in_specs=in_specs, out_specs=out_specs, check_vma=False)
```

```python
import math

import jax
import jax.numpy as jnp
from jax import lax
from jax.sharding import PartitionSpec as P


def combined_all(value, axis, join):
    pieces = jax.tree.map(lambda part: lax.all_gather(part, axis), value)
    head = jax.tree.map(lambda part: part[0], pieces)
    tail = jax.tree.map(lambda part: part[1:], pieces)
    total, _ = lax.scan(lambda total, piece: (join(total, piece), None), head, tail)
    return total


def codes_for(keep_block, count_block, score_block, lengths, block_index):
    requests, block_rows = keep_block.shape
    low = 32
    high = block_rows // low
    places = jnp.arange(block_rows, dtype=jnp.int32)[None, :]
    counted = (places < count_block[:, None])[..., None]
    starts = low * jnp.arange(high, dtype=jnp.int32)
    keep = keep_block[..., None]
    upper = ((keep >= starts) & (keep < starts + low) & counted).astype(jnp.bfloat16)
    lower = (((keep - jnp.arange(low, dtype=jnp.int32)) & (low - 1)) == 0).astype(jnp.bfloat16)
    kept = jnp.einsum("rpa,rpb->rab", upper, lower, preferred_element_type=jnp.float32)
    kept_rows = kept.reshape(requests, block_rows) > 0.5
    position = block_index * block_rows + jnp.arange(block_rows, dtype=jnp.int32)
    valid_rows = position[None, :] < lengths[:, None]
    return jnp.where(valid_rows & kept_rows, -1.0, jnp.where(valid_rows, score_block, 0.0))


def raw_scores(block_data, queries_h):
    head_dim = queries_h.shape[-1]
    factor = 1.0 / math.sqrt(head_dim)
    scores_qk = jnp.einsum(
        "rhc,rbc->rhb",
        queries_h,
        block_data[..., :head_dim],
        preferred_element_type=jnp.float32,
    )
    return lax.optimization_barrier(scores_qk * factor)


def block_partial(block_data, codes, queries_h, scores_qk):
    head_dim = queries_h.shape[-1]
    kept_rows = codes < 0.0
    weight = jnp.maximum(codes, 0.0)
    totals = jnp.sum(weight, axis=1)
    has_merged = totals > 0.0
    floored = jnp.maximum(totals, 1.0)
    shares = (weight / floored[:, None]).astype(jnp.bfloat16)
    merged_score = jnp.sum(shares.astype(jnp.float32)[:, None, :] * scores_qk, axis=-1)
    merged_score = merged_score + jnp.log(floored)[:, None]
    merged_score = jnp.where(has_merged[:, None], merged_score, -1e30)
    scores_qk = jnp.where(kept_rows[:, None, :], scores_qk, -1e30)
    peaks = jnp.maximum(jnp.max(scores_qk, axis=-1), merged_score)
    probs = jnp.where(kept_rows[:, None, :], jnp.exp(scores_qk - peaks[..., None]), 0.0)
    merged_prob = jnp.where(has_merged[:, None], jnp.exp(merged_score - peaks), 0.0)
    mass = jnp.sum(probs, axis=-1) + merged_prob
    rows = jnp.concatenate([shares[:, None, :], probs.astype(jnp.bfloat16)], axis=1)
    products = jnp.einsum(
        "rkb,rbc->rkc", rows, block_data[..., head_dim:], preferred_element_type=jnp.float32
    )
    merged_value = products[:, 0, :].astype(jnp.bfloat16).astype(jnp.float32)
    weighted = (
        products[:, 1:, :]
        + merged_prob.astype(jnp.bfloat16).astype(jnp.float32)[..., None] * merged_value[:, None, :]
    )
    return (peaks, mass, weighted)


def route_tables(offsets, devices, capacity):
    requests = offsets.shape[0]
    index = jnp.arange(requests, dtype=jnp.int32)
    same = offsets[:, None] == offsets[None, :]
    position = jnp.sum((same & (index[None, :] < index[:, None])).astype(jnp.int32), axis=1)
    return position


def pack_slots(values, offsets, device, devices, capacity):
    requests = offsets.shape[0]
    index = jnp.arange(requests, dtype=jnp.int32)
    slot_ids = jnp.arange(devices * capacity, dtype=jnp.int32)
    amount = (slot_ids // capacity - device) % devices
    second = (slot_ids % capacity) == 1
    same = offsets[:, None] == offsets[None, :]
    earlier = jnp.sum((same & (index[None, :] < index[:, None])).astype(jnp.int32), axis=1)
    match = (
        (offsets[None, :] == amount[:, None])
        & (amount != 0)[:, None]
        & ((earlier[None, :] == 1) == second[:, None])
    )
    return jnp.dot(match.astype(values.dtype), values, precision=lax.Precision.HIGHEST)


def unpack_slots(received, values, offsets, position, device, devices, capacity):
    source = (device - offsets) % devices
    slots = source * capacity + jnp.minimum(position, capacity - 1)
    moving = offsets != 0
    flat = received.reshape(devices * capacity, -1)
    picks = (slots[:, None] == jnp.arange(devices * capacity, dtype=jnp.int32)[None, :]) & moving[:, None]
    taken = jnp.dot(picks.astype(values.dtype), flat, precision=lax.Precision.HIGHEST)
    return taken + jnp.where(moving[:, None], jnp.zeros((), values.dtype), values)


def join_partials(first, second):
    peak_one, mass_one, sum_one = first
    peak_two, mass_two, sum_two = second
    largest = jnp.maximum(peak_one, peak_two)
    scale_one = jnp.exp(peak_one - largest)
    scale_two = jnp.exp(peak_two - largest)
    return (
        largest,
        mass_one * scale_one + mass_two * scale_two,
        sum_one * scale_one[..., None] + sum_two * scale_two[..., None],
    )


def body(kv_cache, keep_lists, kept_counts, drop_scores, lengths, offsets, queries, out_weight):
    devices = lax.axis_size("kv")
    device = lax.axis_index("kv")
    requests, block_rows, width = kv_cache.shape
    head_dim = width // 2
    capacity = (requests // 2 + devices - 2) // (devices - 1)
    per_device = requests // devices
    codes = codes_for(keep_lists, kept_counts[:, 0], drop_scores, lengths, device)
    outgoing = pack_slots(codes, offsets, device, devices, capacity)
    received = lax.all_to_all(outgoing, "kv", split_axis=0, concat_axis=0, tiled=True)
    position = route_tables(offsets, devices, capacity)
    held_codes = unpack_slots(received, codes, offsets, position, device, devices, capacity)
    queries_h = queries.reshape(requests, -1, head_dim)
    heads = queries_h.shape[1]
    scores_qk = raw_scores(kv_cache, queries_h)
    peaks, mass, weighted = block_partial(kv_cache, held_codes, queries_h, scores_qk)
    stats = jnp.concatenate([peaks, mass], axis=1)
    stats = jnp.pad(stats, ((0, 0), (0, head_dim - 2 * heads)))
    payload = jnp.concatenate([weighted, stats[:, None, :]], axis=1)
    gathered = lax.all_to_all(payload, "kv", split_axis=0, concat_axis=0, tiled=True)
    gathered = gathered.reshape(devices, per_device, heads + 1, head_dim)
    sums = gathered[:, :, :heads, :]
    peaks_all = gathered[:, :, heads, :heads]
    mass_all = gathered[:, :, heads, heads : 2 * heads]
    largest = jnp.max(peaks_all, axis=0)
    factors = jnp.exp(peaks_all - largest[None])
    upper = jnp.sum(factors[..., None] * sums, axis=0)
    lower = jnp.sum(factors * mass_all, axis=0)
    attended = (upper / lower[..., None]).astype(jnp.bfloat16).reshape(per_device, -1)
    partial_out = jnp.dot(attended, out_weight, preferred_element_type=jnp.float32)
    groups = lax.axis_size("hd")
    group = lax.axis_index("hd")
    pieces = partial_out.reshape(per_device, groups, -1).transpose(1, 0, 2)
    total = lax.dynamic_index_in_dim(pieces, group, 0, keepdims=False)
    for shift in range(1, groups):
        target = (group + shift) % groups
        piece = lax.dynamic_index_in_dim(pieces, target, 0, keepdims=False)
        pairs = [(i, (i + shift) % groups) for i in range(groups)]
        total = total + lax.ppermute(piece, "hd", pairs)
    return total.astype(jnp.bfloat16)


def solution(mesh):
    in_specs = (
        P(None, "kv", None),
        P(None, "kv"),
        P(None, "kv"),
        P(None, "kv"),
        P(),
        P(),
        P(None, "hd"),
        P("hd", None),
    )
    out_specs = P("kv", "hd")
    return jax.shard_map(body, mesh=mesh, in_specs=in_specs, out_specs=out_specs, check_vma=False)
```

```python
import math

import jax
import jax.numpy as jnp
from jax import lax
from jax.sharding import PartitionSpec as P


def combined_all(value, axis, join):
    pieces = jax.tree.map(lambda part: lax.all_gather(part, axis), value)
    head = jax.tree.map(lambda part: part[0], pieces)
    tail = jax.tree.map(lambda part: part[1:], pieces)
    total, _ = lax.scan(lambda total, piece: (join(total, piece), None), head, tail)
    return total


def codes_for(keep_block, count_block, score_block, lengths, block_index):
    requests, block_rows = keep_block.shape
    low = 32
    high = block_rows // low
    places = jnp.arange(block_rows, dtype=jnp.int32)[None, :]
    counted = (places < count_block[:, None])[..., None]
    starts = low * jnp.arange(high, dtype=jnp.int32)
    keep = keep_block[..., None]
    upper = ((keep >= starts) & (keep < starts + low) & counted).astype(jnp.bfloat16)
    lower = (((keep - jnp.arange(low, dtype=jnp.int32)) & (low - 1)) == 0).astype(jnp.bfloat16)
    kept = jnp.einsum("rpa,rpb->rab", upper, lower, preferred_element_type=jnp.float32)
    kept_rows = kept.reshape(requests, block_rows) > 0.5
    position = block_index * block_rows + jnp.arange(block_rows, dtype=jnp.int32)
    valid_rows = position[None, :] < lengths[:, None]
    return jnp.where(valid_rows & kept_rows, -1.0, jnp.where(valid_rows, score_block, 0.0))


def raw_scores(block_data, queries_h):
    head_dim = queries_h.shape[-1]
    factor = 1.0 / math.sqrt(head_dim)
    scores_qk = jnp.einsum(
        "rhc,rbc->rhb",
        queries_h,
        block_data[..., :head_dim],
        preferred_element_type=jnp.float32,
    )
    return lax.optimization_barrier(scores_qk * factor)


def block_partial(block_data, codes, queries_h, scores_qk):
    head_dim = queries_h.shape[-1]
    kept_rows = codes < 0.0
    weight = jnp.maximum(codes, 0.0)
    totals = jnp.sum(weight, axis=1)
    has_merged = totals > 0.0
    floored = jnp.maximum(totals, 1.0)
    shares = (weight / floored[:, None]).astype(jnp.bfloat16)
    merged_score = jnp.sum(shares.astype(jnp.float32)[:, None, :] * scores_qk, axis=-1)
    merged_score = merged_score + jnp.log(floored)[:, None]
    merged_score = jnp.where(has_merged[:, None], merged_score, -1e30)
    scores_qk = jnp.where(kept_rows[:, None, :], scores_qk, -1e30)
    peaks = jnp.maximum(jnp.max(scores_qk, axis=-1), merged_score)
    probs = jnp.where(kept_rows[:, None, :], jnp.exp(scores_qk - peaks[..., None]), 0.0)
    merged_prob = jnp.where(has_merged[:, None], jnp.exp(merged_score - peaks), 0.0)
    mass = jnp.sum(probs, axis=-1) + merged_prob
    rows = jnp.concatenate([shares[:, None, :], probs.astype(jnp.bfloat16)], axis=1)
    products = jnp.einsum(
        "rkb,rbc->rkc", rows, block_data[..., head_dim:], preferred_element_type=jnp.float32
    )
    merged_value = products[:, 0, :].astype(jnp.bfloat16).astype(jnp.float32)
    weighted = (
        products[:, 1:, :]
        + merged_prob.astype(jnp.bfloat16).astype(jnp.float32)[..., None] * merged_value[:, None, :]
    )
    return (peaks, mass, weighted)


def route_tables(offsets, devices, capacity):
    requests = offsets.shape[0]
    index = jnp.arange(requests, dtype=jnp.int32)
    same = offsets[:, None] == offsets[None, :]
    position = jnp.sum((same & (index[None, :] < index[:, None])).astype(jnp.int32), axis=1)
    return position


def pack_slots(values, offsets, device, devices, capacity):
    requests = offsets.shape[0]
    index = jnp.arange(requests, dtype=jnp.int32)
    slot_ids = jnp.arange(devices * capacity, dtype=jnp.int32)
    amount = (slot_ids // capacity - device) % devices
    second = (slot_ids % capacity) == 1
    same = offsets[:, None] == offsets[None, :]
    earlier = jnp.sum((same & (index[None, :] < index[:, None])).astype(jnp.int32), axis=1)
    match = (
        (offsets[None, :] == amount[:, None])
        & (amount != 0)[:, None]
        & ((earlier[None, :] == 1) == second[:, None])
    )
    return jnp.dot(match.astype(values.dtype), values, precision=lax.Precision.HIGHEST)


def unpack_slots(received, values, offsets, position, device, devices, capacity):
    source = (device - offsets) % devices
    moving = offsets != 0
    flat = received.reshape(devices * capacity, -1)
    slot_ids = jnp.arange(devices * capacity, dtype=jnp.int32)[None, :]
    picks = (
        (source[:, None] == slot_ids // capacity)
        & ((position[:, None] == 1) == (slot_ids % capacity == 1))
        & moving[:, None]
    )
    taken = jnp.dot(picks.astype(values.dtype), flat, precision=lax.Precision.HIGHEST)
    return taken + jnp.where(moving[:, None], jnp.zeros((), values.dtype), values)


def join_partials(first, second):
    peak_one, mass_one, sum_one = first
    peak_two, mass_two, sum_two = second
    largest = jnp.maximum(peak_one, peak_two)
    scale_one = jnp.exp(peak_one - largest)
    scale_two = jnp.exp(peak_two - largest)
    return (
        largest,
        mass_one * scale_one + mass_two * scale_two,
        sum_one * scale_one[..., None] + sum_two * scale_two[..., None],
    )


def body(kv_cache, keep_lists, kept_counts, drop_scores, lengths, offsets, queries, out_weight):
    devices = lax.axis_size("kv")
    device = lax.axis_index("kv")
    requests, block_rows, width = kv_cache.shape
    head_dim = width // 2
    capacity = (requests // 2 + devices - 2) // (devices - 1)
    per_device = requests // devices
    codes = codes_for(keep_lists, kept_counts[:, 0], drop_scores, lengths, device)
    outgoing = pack_slots(codes, offsets, device, devices, capacity)
    received = lax.all_to_all(outgoing, "kv", split_axis=0, concat_axis=0, tiled=True)
    position = route_tables(offsets, devices, capacity)
    held_codes = unpack_slots(received, codes, offsets, position, device, devices, capacity)
    queries_h = queries.reshape(requests, -1, head_dim)
    heads = queries_h.shape[1]
    scores_qk = raw_scores(kv_cache, queries_h)
    peaks, mass, weighted = block_partial(kv_cache, held_codes, queries_h, scores_qk)
    stats = jnp.concatenate([peaks, mass], axis=1)
    stats = jnp.pad(stats, ((0, 0), (0, head_dim - 2 * heads)))
    payload = jnp.concatenate([weighted, stats[:, None, :]], axis=1)
    gathered = lax.all_to_all(payload, "kv", split_axis=0, concat_axis=0, tiled=True)
    gathered = gathered.reshape(devices, per_device, heads + 1, head_dim)
    sums = gathered[:, :, :heads, :]
    peaks_all = gathered[:, :, heads, :heads]
    mass_all = gathered[:, :, heads, heads : 2 * heads]
    largest = jnp.max(peaks_all, axis=0)
    factors = jnp.exp(peaks_all - largest[None])
    upper = jnp.sum(factors[..., None] * sums, axis=0)
    lower = jnp.sum(factors * mass_all, axis=0)
    attended = (upper / lower[..., None]).astype(jnp.bfloat16).reshape(per_device, -1)
    partial_out = jnp.dot(attended, out_weight, preferred_element_type=jnp.float32)
    groups = lax.axis_size("hd")
    group = lax.axis_index("hd")
    pieces = partial_out.reshape(per_device, groups, -1).transpose(1, 0, 2)
    total = lax.dynamic_index_in_dim(pieces, group, 0, keepdims=False)
    for shift in range(1, groups):
        target = (group + shift) % groups
        piece = lax.dynamic_index_in_dim(pieces, target, 0, keepdims=False)
        pairs = [(i, (i + shift) % groups) for i in range(groups)]
        total = total + lax.ppermute(piece, "hd", pairs)
    return total.astype(jnp.bfloat16)


def solution(mesh):
    in_specs = (
        P(None, "kv", None),
        P(None, "kv"),
        P(None, "kv"),
        P(None, "kv"),
        P(),
        P(),
        P(None, "hd"),
        P("hd", None),
    )
    out_specs = P("kv", "hd")
    return jax.shard_map(body, mesh=mesh, in_specs=in_specs, out_specs=out_specs, check_vma=False)
```
